32 devices in a mesh: bin: 2 (over y), row: 4 (over x, core), col: 4 (over z).
Axes of the slice: x: 2, y: 2, z: 4, core: 2. Of those that a mesh axis runs over, the one named last changes fastest.
Arguments:
- snapshots: bfloat16 [4096, 16, 64], P('row', 'bin', 'col'), may hold values from -6 to 6
- focus_in: bfloat16 [16, 4096, 128], P('bin', 'row'), may hold values from -0.09375 to 0.09375
- focus_out: bfloat16 [16, 4096, 128], P('bin', 'row'), may hold values from -0.5 to 0.5
- start_basis: float32 [4096, 128], replicated, may hold values from -6 to 6
Outputs:
- covariance: float32 [4096, 4096], P('col', 'row')
- basis_out: float32 [4096, 128], P(('row', 'col'))
The draws below stay inside these ranges and needn't reach their ends.
All inputs are finite; a program needn't handle non-finite values.
Results may differ from the reference program's by a relative error of at most 0.0045.
Values may be sent and summed in bfloat16 or wider, within the bound.
No kernel may reach another device: no remote copies, remote signals or barrier semaphores. Data moves between devices by JAX's collectives and lax.ppermute only.
A program may use at most 128 MiB of HBM per device.

```python
import math
import jax
import jax.numpy as jnp
from jax import lax

M = 4096
R = 128
K = 128
S = 64
ITERS = 2
NBINS = 16


def block_levels(own_key, dims, pieces, low, largest):
    def one(dim, shards_of):
        draws = jax.random.uniform(jax.random.fold_in(jax.random.fold_in(own_key, 6), dim), (shards_of,), jnp.float32, low / len(pieces), largest / len(pieces))
        return jnp.repeat(jnp.exp(draws), dims[dim] // shards_of).reshape((-1,) + (1,) * (len(dims) - dim - 1))

    gain = one(*pieces[0])
    for cut in pieces[1:]:
        gain = gain * one(*cut)
    return gain


def noise(rng, extent, deviation, reach, split=(), dtype=jnp.bfloat16):
    level = block_levels(rng, extent, split, -0.22, 0.18) if split else 1.0
    entries = jax.random.normal(rng, extent, jnp.float32) * deviation * level
    return jnp.minimum(jnp.maximum(entries, -reach), reach).astype(dtype)


def setup_inputs(seed: int = 0) -> dict:
    seeds = jax.random.split(jax.random.key(seed), 5)
    snapshots = noise(seeds[0], (M, NBINS, S), 1.0, 6.0, ((0, 4), (1, 2), (2, 4)))
    focus_in = noise(seeds[1], (NBINS, M, R), M ** -0.5, 0.09375, ((0, 2), (1, 4)))
    focus_out = noise(seeds[2], (NBINS, M, R), R ** -0.5, 0.5, ((0, 2), (1, 4)))
    start_basis = noise(seeds[3], (M, K), 1.0, 6.0, (), jnp.float32)
    return dict(snapshots=snapshots, focus_in=focus_in, focus_out=focus_out, start_basis=start_basis)


def reference(snapshots, focus_in, focus_out, start_basis):
    projected = jnp.einsum('mbs,bmr->brs', snapshots.astype(jnp.float32), focus_in.astype(jnp.float32), precision=lax.Precision.HIGHEST).astype(jnp.bfloat16)
    lifted = jnp.einsum('bmr,brs->mbs', focus_out.astype(jnp.float32), projected.astype(jnp.float32), precision=lax.Precision.HIGHEST)
    focused = (snapshots.astype(jnp.float32) + lifted).astype(jnp.bfloat16)
    flattened = focused.reshape(M, NBINS * S).astype(jnp.float32)
    covariance = jnp.dot(flattened.astype(jnp.float32), flattened.T.astype(jnp.float32), precision=lax.Precision.HIGHEST, preferred_element_type=jnp.float32) * (1.0 / (NBINS * S))
    basis_now = start_basis
    for sweep_index in range(ITERS):
        image = jnp.dot(covariance.astype(jnp.float32), basis_now.astype(jnp.float32), precision=lax.Precision.HIGHEST, preferred_element_type=jnp.float32)
        gram_matrix = jnp.dot(image.T.astype(jnp.float32), image.astype(jnp.float32), precision=lax.Precision.HIGHEST, preferred_element_type=jnp.float32)
        lower_factor = jnp.linalg.cholesky(gram_matrix)
        basis_now = jax.scipy.linalg.solve_triangular(lower_factor, image.T, lower=True).T
    return (covariance, basis_now * math.sqrt(M))
```

```python
import math

import jax
import jax.numpy as jnp
from jax import lax
from jax.sharding import PartitionSpec as P

ITERS = 2


def _transpose_pairs(row_count, col_count):
    return [
        (i * col_count + j, j * row_count + i)
        for i in range(row_count)
        for j in range(col_count)
        if i != j
    ]


def _qr_step(image, gram_axis):
    gram_part = jnp.dot(
        image.T, image, precision=lax.Precision.HIGHEST, preferred_element_type=jnp.float32
    )
    gram_matrix = lax.psum(gram_part, gram_axis)
    lower_factor = jnp.linalg.cholesky(gram_matrix)
    return jax.scipy.linalg.solve_triangular(lower_factor, image.T, lower=True).T


def shards(snapshots, focus_in, focus_out, start_basis):
    rows_here, bins_here, snaps_here = snapshots.shape
    bin_count = lax.axis_size("bin")
    row_count = lax.axis_size("row")
    col_count = lax.axis_size("col")
    col_here = lax.axis_index("col")
    row_here = lax.axis_index("row")
    partial_proj = jnp.einsum(
        "mbs,bmr->brs", snapshots, focus_in, preferred_element_type=jnp.float32
    )
    projected = lax.psum(partial_proj, "row").astype(jnp.bfloat16)
    lifted = jnp.einsum("bmr,brs->mbs", focus_out, projected, preferred_element_type=jnp.float32)
    focused = (snapshots.astype(jnp.float32) + lifted).astype(jnp.bfloat16)
    columns = bins_here * snaps_here
    local_rows = focused.reshape(rows_here, columns)
    array_size = rows_here * row_count
    col_block = array_size // col_count
    scaling = 1.0 / (columns * col_count * bin_count)

    right_rows = lax.all_gather(local_rows, ("bin", "col"), axis=0, tiled=False)
    if row_count == col_count:
        swapped = lax.ppermute(local_rows, ("row", "col"), _transpose_pairs(row_count, col_count))
        swapped = jnp.where(row_here == col_here, local_rows, swapped)
        left_rows = lax.all_gather(swapped, ("bin", "row"), axis=0, tiled=False)
    else:
        every_row = lax.all_gather(right_rows, "row", axis=1, tiled=True)
        left_rows = lax.dynamic_slice_in_dim(every_row, col_here * col_block, col_block, 1)
    covariance = lax.dot_general(
        left_rows, right_rows, (((0, 2), (0, 2)), ((), ())), preferred_element_type=jnp.float32
    ) * scaling

    basis_rows = lax.dynamic_slice_in_dim(start_basis, row_here * rows_here, rows_here, 0)
    on_rows = True
    for sweep_index in range(ITERS):
        if on_rows:
            partial_image = jnp.dot(
                covariance, basis_rows, precision=lax.Precision.HIGHEST,
                preferred_element_type=jnp.float32,
            )
            image = lax.psum(partial_image, "row")
            basis_rows = _qr_step(image, "col")
        else:
            partial_image = lax.dot_general(
                covariance, basis_rows, (((0,), (0,)), ((), ())),
                precision=lax.Precision.HIGHEST, preferred_element_type=jnp.float32,
            )
            image = lax.psum(partial_image, "col")
            basis_rows = _qr_step(image, "row")
        on_rows = not on_rows
    if not on_rows:
        swapped = lax.ppermute(basis_rows, ("row", "col"), _transpose_pairs(row_count, col_count))
        basis_rows = jnp.where(row_here == col_here, basis_rows, swapped)
    out_rows = array_size // (row_count * col_count)
    basis_out = lax.dynamic_slice_in_dim(basis_rows, col_here * out_rows, out_rows, 0) * math.sqrt(array_size)
    return (covariance, basis_out)


def solution(mesh):
    in_specs = (P("row", "bin", "col"), P("bin", "row", None), P("bin", "row", None), P())
    out_specs = (P("col", "row"), P(("row", "col"), None))
    return jax.shard_map(shards, mesh=mesh, in_specs=in_specs, out_specs=out_specs, check_vma=False)
```

```python
import math

import jax
import jax.numpy as jnp
from jax import lax
from jax.sharding import PartitionSpec as P

ITERS = 2


def _transpose_pairs(row_count, col_count):
    return [
        (i * col_count + j, j * row_count + i)
        for i in range(row_count)
        for j in range(col_count)
        if i != j
    ]


def _butterfly_sum(x, axis):
    count = lax.axis_size(axis)
    if count & (count - 1):
        return lax.psum(x, axis)
    step = 1
    while step < count:
        x = x + lax.ppermute(x, axis, [(i, i ^ step) for i in range(count)])
        step *= 2
    return x


def _butterfly_gather(x, axes):
    x = x[None]
    for axis in axes:
        count = lax.axis_size(axis)
        if count & (count - 1):
            x = lax.all_gather(x, axis, axis=0, tiled=False)
            x = x.reshape((-1,) + x.shape[2:])
            continue
        here = lax.axis_index(axis)
        step = 1
        while step < count:
            other = lax.ppermute(x, axis, [(i, i ^ step) for i in range(count)])
            low = (here & step) == 0
            x = jnp.where(low, jnp.concatenate([x, other], 0), jnp.concatenate([other, x], 0))
            step *= 2
    return x


def _qr_step(image, gram_axis):
    gram_part = jnp.dot(
        image.T, image, precision=lax.Precision.HIGHEST, preferred_element_type=jnp.float32
    )
    gram_matrix = _butterfly_sum(gram_part, gram_axis)
    lower_factor = jnp.linalg.cholesky(gram_matrix)
    return jax.scipy.linalg.solve_triangular(lower_factor, image.T, lower=True).T


def shards(snapshots, focus_in, focus_out, start_basis):
    rows_here, bins_here, snaps_here = snapshots.shape
    bin_count = lax.axis_size("bin")
    row_count = lax.axis_size("row")
    col_count = lax.axis_size("col")
    col_here = lax.axis_index("col")
    row_here = lax.axis_index("row")
    partial_proj = jnp.einsum(
        "mbs,bmr->brs", snapshots, focus_in, preferred_element_type=jnp.float32
    )
    projected = _butterfly_sum(partial_proj, "row").astype(jnp.bfloat16)
    lifted = jnp.einsum("bmr,brs->mbs", focus_out, projected, preferred_element_type=jnp.float32)
    focused = (snapshots.astype(jnp.float32) + lifted).astype(jnp.bfloat16)
    columns = bins_here * snaps_here
    local_rows = focused.reshape(rows_here, columns)
    array_size = rows_here * row_count
    col_block = array_size // col_count
    scaling = 1.0 / (columns * col_count * bin_count)

    right_rows = _butterfly_gather(local_rows, ("bin", "col"))
    if row_count == col_count:
        swapped = lax.ppermute(local_rows, ("row", "col"), _transpose_pairs(row_count, col_count))
        swapped = jnp.where(row_here == col_here, local_rows, swapped)
        left_rows = _butterfly_gather(swapped, ("bin", "row"))
    else:
        every_row = lax.all_gather(right_rows, "row", axis=1, tiled=True)
        left_rows = lax.dynamic_slice_in_dim(every_row, col_here * col_block, col_block, 1)
    covariance = lax.dot_general(
        left_rows, right_rows, (((0, 2), (0, 2)), ((), ())), preferred_element_type=jnp.float32
    ) * scaling

    basis_rows = lax.dynamic_slice_in_dim(start_basis, row_here * rows_here, rows_here, 0)
    on_rows = True
    for sweep_index in range(ITERS):
        if on_rows:
            partial_image = jnp.dot(
                covariance, basis_rows, precision=lax.Precision.HIGHEST,
                preferred_element_type=jnp.float32,
            )
            image = _butterfly_sum(partial_image, "row")
            basis_rows = _qr_step(image, "col")
        else:
            partial_image = lax.dot_general(
                covariance, basis_rows, (((0,), (0,)), ((), ())),
                precision=lax.Precision.HIGHEST, preferred_element_type=jnp.float32,
            )
            image = _butterfly_sum(partial_image, "col")
            basis_rows = _qr_step(image, "row")
        on_rows = not on_rows
    if not on_rows:
        swapped = lax.ppermute(basis_rows, ("row", "col"), _transpose_pairs(row_count, col_count))
        basis_rows = jnp.where(row_here == col_here, basis_rows, swapped)
    out_rows = array_size // (row_count * col_count)
    basis_out = lax.dynamic_slice_in_dim(basis_rows, col_here * out_rows, out_rows, 0) * math.sqrt(array_size)
    return (covariance, basis_out)


def solution(mesh):
    in_specs = (P("row", "bin", "col"), P("bin", "row", None), P("bin", "row", None), P())
    out_specs = (P("col", "row"), P(("row", "col"), None))
    return jax.shard_map(shards, mesh=mesh, in_specs=in_specs, out_specs=out_specs, check_vma=False)
```

```python
import math

import jax
import jax.numpy as jnp
from jax import lax
from jax.sharding import PartitionSpec as P

ITERS = 2


def _transpose_pairs(row_count, col_count):
    return [
        (i * col_count + j, j * row_count + i)
        for i in range(row_count)
        for j in range(col_count)
        if i != j
    ]


def _butterfly_sum(x, axis):
    count = lax.axis_size(axis)
    if count & (count - 1):
        return lax.psum(x, axis)
    step = 1
    while step < count:
        x = x + lax.ppermute(x, axis, [(i, i ^ step) for i in range(count)])
        step *= 2
    return x


def _bits(count, far_first):
    steps = []
    step = 1
    while step < count:
        steps.append(step)
        step *= 2
    return steps[::-1] if far_first else steps


def _butterfly_gather(x, axes):
    x = x[None]
    for axis in axes:
        count = lax.axis_size(axis)
        if count & (count - 1):
            x = lax.all_gather(x, axis, axis=0, tiled=False)
            x = x.reshape((-1,) + x.shape[2:])
            continue
        here = lax.axis_index(axis)
        for step in _bits(count, True):
            other = lax.ppermute(x, axis, [(i, i ^ step) for i in range(count)])
            low = (here & step) == 0
            x = jnp.where(low, jnp.concatenate([x, other], 0), jnp.concatenate([other, x], 0))
    return x


def _halving_sum(x, axis):
    count = lax.axis_size(axis)
    if count & (count - 1) or x.shape[0] % count:
        return _butterfly_sum(x, axis)
    here = lax.axis_index(axis)
    steps = _bits(count, False)
    for step in steps:
        half = x.shape[0] // 2
        low = (here & step) == 0
        keep = jnp.where(low, x[:half], x[half:])
        give = jnp.where(low, x[half:], x[:half])
        x = keep + lax.ppermute(give, axis, [(i, i ^ step) for i in range(count)])
    for step in steps[::-1]:
        low = (here & step) == 0
        other = lax.ppermute(x, axis, [(i, i ^ step) for i in range(count)])
        x = jnp.where(low, jnp.concatenate([x, other], 0), jnp.concatenate([other, x], 0))
    return x


def _qr_step(image, gram_axis):
    gram_part = jnp.dot(
        image.T, image, precision=lax.Precision.HIGHEST, preferred_element_type=jnp.float32
    )
    gram_matrix = _butterfly_sum(gram_part, gram_axis)
    lower_factor = jnp.linalg.cholesky(gram_matrix)
    return jax.scipy.linalg.solve_triangular(lower_factor, image.T, lower=True).T


def shards(snapshots, focus_in, focus_out, start_basis):
    rows_here, bins_here, snaps_here = snapshots.shape
    bin_count = lax.axis_size("bin")
    row_count = lax.axis_size("row")
    col_count = lax.axis_size("col")
    col_here = lax.axis_index("col")
    row_here = lax.axis_index("row")
    partial_proj = jnp.einsum(
        "mbs,bmr->brs", snapshots, focus_in, preferred_element_type=jnp.float32
    )
    projected = _butterfly_sum(partial_proj, "row").astype(jnp.bfloat16)
    lifted = jnp.einsum("bmr,brs->mbs", focus_out, projected, preferred_element_type=jnp.float32)
    focused = (snapshots.astype(jnp.float32) + lifted).astype(jnp.bfloat16)
    columns = bins_here * snaps_here
    local_rows = focused.reshape(rows_here, columns)
    array_size = rows_here * row_count
    col_block = array_size // col_count
    scaling = 1.0 / (columns * col_count * bin_count)

    right_rows = _butterfly_gather(local_rows, ("bin", "col"))
    if row_count == col_count:
        swapped = lax.ppermute(local_rows, ("row", "col"), _transpose_pairs(row_count, col_count))
        swapped = jnp.where(row_here == col_here, local_rows, swapped)
        left_rows = _butterfly_gather(swapped, ("bin", "row"))
    else:
        every_row = lax.all_gather(right_rows, "row", axis=1, tiled=True)
        left_rows = lax.dynamic_slice_in_dim(every_row, col_here * col_block, col_block, 1)
    covariance = lax.dot_general(
        left_rows, right_rows, (((0, 2), (0, 2)), ((), ())), preferred_element_type=jnp.float32
    ) * scaling

    basis_rows = lax.dynamic_slice_in_dim(start_basis, row_here * rows_here, rows_here, 0)
    on_rows = True
    for sweep_index in range(ITERS):
        if on_rows:
            partial_image = jnp.dot(
                covariance, basis_rows, precision=lax.Precision.HIGHEST,
                preferred_element_type=jnp.float32,
            )
            image = _butterfly_sum(partial_image, "row")
            basis_rows = _qr_step(image, "col")
        else:
            partial_image = lax.dot_general(
                covariance, basis_rows, (((0,), (0,)), ((), ())),
                precision=lax.Precision.HIGHEST, preferred_element_type=jnp.float32,
            )
            image = _halving_sum(partial_image, "col")
            basis_rows = _qr_step(image, "row")
        on_rows = not on_rows
    if not on_rows:
        swapped = lax.ppermute(basis_rows, ("row", "col"), _transpose_pairs(row_count, col_count))
        basis_rows = jnp.where(row_here == col_here, basis_rows, swapped)
    out_rows = array_size // (row_count * col_count)
    basis_out = lax.dynamic_slice_in_dim(basis_rows, col_here * out_rows, out_rows, 0) * math.sqrt(array_size)
    return (covariance, basis_out)


def solution(mesh):
    in_specs = (P("row", "bin", "col"), P("bin", "row", None), P("bin", "row", None), P())
    out_specs = (P("col", "row"), P(("row", "col"), None))
    return jax.shard_map(shards, mesh=mesh, in_specs=in_specs, out_specs=out_specs, check_vma=False)
```

```python
import math

import jax
import jax.numpy as jnp
from jax import lax
from jax.sharding import PartitionSpec as P

ITERS = 2


def _transpose_pairs(row_count, col_count):
    return [
        (i * col_count + j, j * row_count + i)
        for i in range(row_count)
        for j in range(col_count)
        if i != j
    ]


def _butterfly_sum(x, axis):
    count = lax.axis_size(axis)
    if count & (count - 1):
        return lax.psum(x, axis)
    step = 1
    while step < count:
        x = x + lax.ppermute(x, axis, [(i, i ^ step) for i in range(count)])
        step *= 2
    return x


def _bits(count, far_first):
    steps = []
    step = 1
    while step < count:
        steps.append(step)
        step *= 2
    return steps[::-1] if far_first else steps


def _plan(axes):
    steps = []
    for axis in axes:
        steps += [(axis, step) for step in _bits(lax.axis_size(axis), True)]
    return steps


def _butterfly_gather(x, plan):
    x = x[None]
    for axis, step in plan:
        count = lax.axis_size(axis)
        here = lax.axis_index(axis)
        other = lax.ppermute(x, axis, [(i, i ^ step) for i in range(count)])
        low = (here & step) == 0
        x = jnp.where(low, jnp.concatenate([x, other], 0), jnp.concatenate([other, x], 0))
    return x


def _keys(plan, rename):
    keys = []
    for index in range(2 ** len(plan)):
        key = {}
        for bit, (axis, step) in enumerate(plan):
            name = rename.get(axis, axis)
            key[name] = key.get(name, 0) + (step if index >> bit & 1 else 0)
        keys.append(tuple(sorted(key.items())))
    return keys


def _halving_sum(x, axis):
    count = lax.axis_size(axis)
    if count & (count - 1) or x.shape[0] % count:
        return _butterfly_sum(x, axis)
    here = lax.axis_index(axis)
    steps = _bits(count, False)
    for step in steps:
        half = x.shape[0] // 2
        low = (here & step) == 0
        keep = jnp.where(low, x[:half], x[half:])
        give = jnp.where(low, x[half:], x[:half])
        x = keep + lax.ppermute(give, axis, [(i, i ^ step) for i in range(count)])
    for step in steps[::-1]:
        low = (here & step) == 0
        other = lax.ppermute(x, axis, [(i, i ^ step) for i in range(count)])
        x = jnp.where(low, jnp.concatenate([x, other], 0), jnp.concatenate([other, x], 0))
    return x


def _qr_step(image, gram_axis):
    gram_part = jnp.dot(
        image.T, image, precision=lax.Precision.HIGHEST, preferred_element_type=jnp.float32
    )
    gram_matrix = _butterfly_sum(gram_part, gram_axis)
    lower_factor = jnp.linalg.cholesky(gram_matrix)
    return jax.scipy.linalg.solve_triangular(lower_factor, image.T, lower=True).T


def shards(snapshots, focus_in, focus_out, start_basis):
    rows_here, bins_here, snaps_here = snapshots.shape
    bin_count = lax.axis_size("bin")
    row_count = lax.axis_size("row")
    col_count = lax.axis_size("col")
    col_here = lax.axis_index("col")
    row_here = lax.axis_index("row")
    partial_proj = jnp.einsum(
        "mbs,bmr->brs", snapshots, focus_in, preferred_element_type=jnp.float32
    )
    projected = _butterfly_sum(partial_proj, "row").astype(jnp.bfloat16)
    lifted = jnp.einsum("bmr,brs->mbs", focus_out, projected, preferred_element_type=jnp.float32)
    focused = (snapshots.astype(jnp.float32) + lifted).astype(jnp.bfloat16)
    columns = bins_here * snaps_here
    local_rows = focused.reshape(rows_here, columns)
    array_size = rows_here * row_count
    col_block = array_size // col_count
    scaling = 1.0 / (columns * col_count * bin_count)

    power_of_two = all(n & (n - 1) == 0 for n in (bin_count, row_count, col_count))
    if row_count == col_count and power_of_two:
        right_plan = _plan(("col", "bin"))
        left_plan = _plan(("bin", "row"))
        right_rows = _butterfly_gather(local_rows, right_plan)
        swapped = lax.ppermute(local_rows, ("row", "col"), _transpose_pairs(row_count, col_count))
        swapped = jnp.where(row_here == col_here, local_rows, swapped)
        left_rows = _butterfly_gather(swapped, left_plan)
        left_keys = _keys(left_plan, {"row": "col"})
        order = [left_keys.index(key) for key in _keys(right_plan, {})]
        left_rows = jnp.stack([left_rows[j] for j in order])
    else:
        right_rows = lax.all_gather(local_rows, ("bin", "col"), axis=0, tiled=False)
        every_row = lax.all_gather(right_rows, "row", axis=1, tiled=True)
        left_rows = lax.dynamic_slice_in_dim(every_row, col_here * col_block, col_block, 1)
    covariance = lax.dot_general(
        left_rows, right_rows, (((0, 2), (0, 2)), ((), ())), preferred_element_type=jnp.float32
    ) * scaling

    basis_rows = lax.dynamic_slice_in_dim(start_basis, row_here * rows_here, rows_here, 0)
    on_rows = True
    for sweep_index in range(ITERS):
        if on_rows:
            partial_image = jnp.dot(
                covariance, basis_rows, precision=lax.Precision.HIGHEST,
                preferred_element_type=jnp.float32,
            )
            image = _butterfly_sum(partial_image, "row")
            basis_rows = _qr_step(image, "col")
        else:
            partial_image = lax.dot_general(
                covariance, basis_rows, (((0,), (0,)), ((), ())),
                precision=lax.Precision.HIGHEST, preferred_element_type=jnp.float32,
            )
            image = _halving_sum(partial_image, "col")
            basis_rows = _qr_step(image, "row")
        on_rows = not on_rows
    if not on_rows:
        swapped = lax.ppermute(basis_rows, ("row", "col"), _transpose_pairs(row_count, col_count))
        basis_rows = jnp.where(row_here == col_here, basis_rows, swapped)
    out_rows = array_size // (row_count * col_count)
    basis_out = lax.dynamic_slice_in_dim(basis_rows, col_here * out_rows, out_rows, 0) * math.sqrt(array_size)
    return (covariance, basis_out)


def solution(mesh):
    in_specs = (P("row", "bin", "col"), P("bin", "row", None), P("bin", "row", None), P())
    out_specs = (P("col", "row"), P(("row", "col"), None))
    return jax.shard_map(shards, mesh=mesh, in_specs=in_specs, out_specs=out_specs, check_vma=False)
```

```python
import math

import jax
import jax.numpy as jnp
from jax import lax
from jax.sharding import PartitionSpec as P

ITERS = 2


def _transpose_pairs(row_count, col_count):
    return [
        (i * col_count + j, j * row_count + i)
        for i in range(row_count)
        for j in range(col_count)
        if i != j
    ]


def _butterfly_sum(x, axis):
    count = lax.axis_size(axis)
    if count & (count - 1):
        return lax.psum(x, axis)
    step = 1
    while step < count:
        x = x + lax.ppermute(x, axis, [(i, i ^ step) for i in range(count)])
        step *= 2
    return x


def _bits(count, far_first):
    steps = []
    step = 1
    while step < count:
        steps.append(step)
        step *= 2
    return steps[::-1] if far_first else steps


def _plan(axes):
    steps = []
    for axis in axes:
        steps += [(axis, step) for step in _bits(lax.axis_size(axis), True)]
    return steps


def _butterfly_gather(x, plan):
    x = x[None]
    for axis, step in plan:
        count = lax.axis_size(axis)
        here = lax.axis_index(axis)
        other = lax.ppermute(x, axis, [(i, i ^ step) for i in range(count)])
        low = (here & step) == 0
        x = jnp.where(low, jnp.concatenate([x, other], 0), jnp.concatenate([other, x], 0))
    return x


def _keys(plan, rename):
    keys = []
    for index in range(2 ** len(plan)):
        key = {}
        for bit, (axis, step) in enumerate(plan):
            name = rename.get(axis, axis)
            key[name] = key.get(name, 0) + (step if index >> bit & 1 else 0)
        keys.append(tuple(sorted(key.items())))
    return keys


def _halving_sum(x, axis):
    count = lax.axis_size(axis)
    if count & (count - 1) or x.shape[0] % count:
        return _butterfly_sum(x, axis)
    here = lax.axis_index(axis)
    steps = _bits(count, False)
    for step in steps:
        half = x.shape[0] // 2
        low = (here & step) == 0
        keep = jnp.where(low, x[:half], x[half:])
        give = jnp.where(low, x[half:], x[:half])
        x = keep + lax.ppermute(give, axis, [(i, i ^ step) for i in range(count)])
    for step in steps[::-1]:
        low = (here & step) == 0
        other = lax.ppermute(x, axis, [(i, i ^ step) for i in range(count)])
        x = jnp.where(low, jnp.concatenate([x, other], 0), jnp.concatenate([other, x], 0))
    return x


def _qr_step(image, gram_axis):
    gram_part = jnp.dot(
        image.T, image, precision=lax.Precision.HIGHEST, preferred_element_type=jnp.float32
    )
    gram_matrix = _butterfly_sum(gram_part, gram_axis)
    lower_factor = jnp.linalg.cholesky(gram_matrix)
    return jax.scipy.linalg.solve_triangular(lower_factor, image.T, lower=True).T


def shards(snapshots, focus_in, focus_out, start_basis):
    rows_here, bins_here, snaps_here = snapshots.shape
    bin_count = lax.axis_size("bin")
    row_count = lax.axis_size("row")
    col_count = lax.axis_size("col")
    col_here = lax.axis_index("col")
    row_here = lax.axis_index("row")
    partial_proj = jnp.einsum(
        "mbs,bmr->brs", snapshots, focus_in, preferred_element_type=jnp.float32
    )
    projected = _butterfly_sum(partial_proj, "row").astype(jnp.bfloat16)
    lifted = jnp.einsum("bmr,brs->mbs", focus_out, projected, preferred_element_type=jnp.float32)
    focused = (snapshots.astype(jnp.float32) + lifted).astype(jnp.bfloat16)
    columns = bins_here * snaps_here
    local_rows = focused.reshape(rows_here, columns)
    array_size = rows_here * row_count
    col_block = array_size // col_count
    scaling = 1.0 / (columns * col_count * bin_count)

    power_of_two = all(n & (n - 1) == 0 for n in (bin_count, row_count, col_count))
    if row_count == col_count and power_of_two:
        left_plan = _plan(("bin", "row"))
        right_rows = lax.all_gather(local_rows, ("bin", "col"), axis=0, tiled=False)
        right_rows = right_rows.reshape((-1,) + local_rows.shape)
        swapped = lax.ppermute(local_rows, ("row", "col"), _transpose_pairs(row_count, col_count))
        swapped = jnp.where(row_here == col_here, local_rows, swapped)
        left_rows = _butterfly_gather(swapped, left_plan)
        left_keys = _keys(left_plan, {"row": "col"})
        right_keys = [
            (("bin", i // col_count), ("col", i % col_count)) for i in range(bin_count * col_count)
        ]
        order = [left_keys.index(key) for key in right_keys]
        left_rows = jnp.stack([left_rows[j] for j in order])
    else:
        right_rows = lax.all_gather(local_rows, ("bin", "col"), axis=0, tiled=False)
        every_row = lax.all_gather(right_rows, "row", axis=1, tiled=True)
        left_rows = lax.dynamic_slice_in_dim(every_row, col_here * col_block, col_block, 1)
    covariance = lax.dot_general(
        left_rows, right_rows, (((0, 2), (0, 2)), ((), ())), preferred_element_type=jnp.float32
    ) * scaling

    basis_rows = lax.dynamic_slice_in_dim(start_basis, row_here * rows_here, rows_here, 0)
    on_rows = True
    for sweep_index in range(ITERS):
        if on_rows:
            partial_image = jnp.dot(
                covariance, basis_rows, precision=lax.Precision.HIGHEST,
                preferred_element_type=jnp.float32,
            )
            image = _butterfly_sum(partial_image, "row")
            basis_rows = _qr_step(image, "col")
        else:
            partial_image = lax.dot_general(
                covariance, basis_rows, (((0,), (0,)), ((), ())),
                precision=lax.Precision.HIGHEST, preferred_element_type=jnp.float32,
            )
            image = _halving_sum(partial_image, "col")
            basis_rows = _qr_step(image, "row")
        on_rows = not on_rows
    if not on_rows:
        swapped = lax.ppermute(basis_rows, ("row", "col"), _transpose_pairs(row_count, col_count))
        basis_rows = jnp.where(row_here == col_here, basis_rows, swapped)
    out_rows = array_size // (row_count * col_count)
    basis_out = lax.dynamic_slice_in_dim(basis_rows, col_here * out_rows, out_rows, 0) * math.sqrt(array_size)
    return (covariance, basis_out)


def solution(mesh):
    in_specs = (P("row", "bin", "col"), P("bin", "row", None), P("bin", "row", None), P())
    out_specs = (P("col", "row"), P(("row", "col"), None))
    return jax.shard_map(shards, mesh=mesh, in_specs=in_specs, out_specs=out_specs, check_vma=False)
```

```python
import math

import jax
import jax.numpy as jnp
from jax import lax
from jax.sharding import PartitionSpec as P

ITERS = 2


def _transpose_pairs(row_count, col_count):
    return [
        (i * col_count + j, j * row_count + i)
        for i in range(row_count)
        for j in range(col_count)
        if i != j
    ]


def _butterfly_sum(x, axis):
    count = lax.axis_size(axis)
    if count & (count - 1):
        return lax.psum(x, axis)
    step = 1
    while step < count:
        x = x + lax.ppermute(x, axis, [(i, i ^ step) for i in range(count)])
        step *= 2
    return x


def _bits(count, far_first):
    steps = []
    step = 1
    while step < count:
        steps.append(step)
        step *= 2
    return steps[::-1] if far_first else steps


def _direct_sum(x, axis):
    count = lax.axis_size(axis)
    if count != 4:
        return _butterfly_sum(x, axis)
    got = [lax.ppermute(x, axis, [(i, i ^ k) for i in range(count)]) for k in (1, 2, 3)]
    return (x + got[0]) + (got[1] + got[2])


def _butterfly_gather(xs, axes_of):
    xs = [x[None] for x in xs]
    plans = [[(axis, step) for axis in axes for step in _bits(lax.axis_size(axis), True)] for axes in axes_of]
    while any(plans):
        head = next(plan[0] for plan in plans if plan)
        which = [k for k, plan in enumerate(plans) if plan and plan[0] == head]
        axis, step = head
        count = lax.axis_size(axis)
        low = (lax.axis_index(axis) & step) == 0
        others = lax.ppermute([xs[k] for k in which], axis, [(i, i ^ step) for i in range(count)])
        for k, other in zip(which, others):
            xs[k] = jnp.where(low, jnp.concatenate([xs[k], other], 0), jnp.concatenate([other, xs[k]], 0))
            plans[k] = plans[k][1:]
    return xs


def _halving_sum(x, axis):
    count = lax.axis_size(axis)
    if count & (count - 1) or x.shape[0] % count:
        return _butterfly_sum(x, axis)
    here = lax.axis_index(axis)
    steps = _bits(count, False)
    for step in steps:
        half = x.shape[0] // 2
        low = (here & step) == 0
        keep = jnp.where(low, x[:half], x[half:])
        give = jnp.where(low, x[half:], x[:half])
        x = keep + lax.ppermute(give, axis, [(i, i ^ step) for i in range(count)])
    for step in steps[::-1]:
        low = (here & step) == 0
        other = lax.ppermute(x, axis, [(i, i ^ step) for i in range(count)])
        x = jnp.where(low, jnp.concatenate([x, other], 0), jnp.concatenate([other, x], 0))
    return x


def _qr_step(image, gram_axis):
    gram_part = jnp.dot(
        image.T, image, precision=lax.Precision.HIGHEST, preferred_element_type=jnp.float32
    )
    gram_matrix = _direct_sum(gram_part, gram_axis)
    lower_factor = jnp.linalg.cholesky(gram_matrix)
    return jax.scipy.linalg.solve_triangular(lower_factor, image.T, lower=True).T


def shards(snapshots, focus_in, focus_out, start_basis):
    rows_here, bins_here, snaps_here = snapshots.shape
    bin_count = lax.axis_size("bin")
    row_count = lax.axis_size("row")
    col_count = lax.axis_size("col")
    col_here = lax.axis_index("col")
    row_here = lax.axis_index("row")
    partial_proj = jnp.einsum(
        "mbs,bmr->brs", snapshots, focus_in, preferred_element_type=jnp.float32
    )
    projected = _direct_sum(partial_proj, "row").astype(jnp.bfloat16)
    lifted = jnp.einsum("bmr,brs->mbs", focus_out, projected, preferred_element_type=jnp.float32)
    focused = (snapshots.astype(jnp.float32) + lifted).astype(jnp.bfloat16)
    columns = bins_here * snaps_here
    local_rows = focused.reshape(rows_here, columns)
    array_size = rows_here * row_count
    col_block = array_size // col_count
    scaling = 1.0 / (columns * col_count * bin_count)

    power_of_two = all(n & (n - 1) == 0 for n in (bin_count, row_count, col_count))
    if row_count == col_count and power_of_two:
        swapped = lax.ppermute(local_rows, ("row", "col"), _transpose_pairs(row_count, col_count))
        swapped = jnp.where(row_here == col_here, local_rows, swapped)
        right_rows, left_rows = _butterfly_gather(
            [local_rows, swapped], [("bin", "col"), ("bin", "row")]
        )
    else:
        right_rows = lax.all_gather(local_rows, ("bin", "col"), axis=0, tiled=False)
        every_row = lax.all_gather(right_rows, "row", axis=1, tiled=True)
        left_rows = lax.dynamic_slice_in_dim(every_row, col_here * col_block, col_block, 1)
    covariance = lax.dot_general(
        left_rows, right_rows, (((0, 2), (0, 2)), ((), ())), preferred_element_type=jnp.float32
    ) * scaling

    basis_rows = lax.dynamic_slice_in_dim(start_basis, row_here * rows_here, rows_here, 0)
    on_rows = True
    for sweep_index in range(ITERS):
        if on_rows:
            partial_image = jnp.dot(
                covariance, basis_rows, precision=lax.Precision.HIGHEST,
                preferred_element_type=jnp.float32,
            )
            image = _butterfly_sum(partial_image, "row")
            basis_rows = _qr_step(image, "col")
        else:
            partial_image = lax.dot_general(
                covariance, basis_rows, (((0,), (0,)), ((), ())),
                precision=lax.Precision.HIGHEST, preferred_element_type=jnp.float32,
            )
            image = _halving_sum(partial_image, "col")
            basis_rows = _qr_step(image, "row")
        on_rows = not on_rows
    if not on_rows:
        swapped = lax.ppermute(basis_rows, ("row", "col"), _transpose_pairs(row_count, col_count))
        basis_rows = jnp.where(row_here == col_here, basis_rows, swapped)
    out_rows = array_size // (row_count * col_count)
    basis_out = lax.dynamic_slice_in_dim(basis_rows, col_here * out_rows, out_rows, 0) * math.sqrt(array_size)
    return (covariance, basis_out)


def solution(mesh):
    in_specs = (P("row", "bin", "col"), P("bin", "row", None), P("bin", "row", None), P())
    out_specs = (P("col", "row"), P(("row", "col"), None))
    return jax.shard_map(shards, mesh=mesh, in_specs=in_specs, out_specs=out_specs, check_vma=False)
```

```python
import math

import jax
import jax.numpy as jnp
from jax import lax
from jax.sharding import PartitionSpec as P

ITERS = 2


def _transpose_pairs(row_count, col_count):
    return [
        (i * col_count + j, j * row_count + i)
        for i in range(row_count)
        for j in range(col_count)
        if i != j
    ]


def _butterfly_sum(x, axis):
    count = lax.axis_size(axis)
    if count & (count - 1):
        return lax.psum(x, axis)
    step = 1
    while step < count:
        x = x + lax.ppermute(x, axis, [(i, i ^ step) for i in range(count)])
        step *= 2
    return x


def _bits(count, far_first):
    steps = []
    step = 1
    while step < count:
        steps.append(step)
        step *= 2
    return steps[::-1] if far_first else steps


def _direct_sum(x, axis):
    count = lax.axis_size(axis)
    if count != 4:
        return _butterfly_sum(x, axis)
    got = [lax.ppermute(x, axis, [(i, i ^ k) for i in range(count)]) for k in (1, 2, 3)]
    return (x + got[0]) + (got[1] + got[2])


def _butterfly_gather(xs, axes_of):
    xs = [x[None] for x in xs]
    plans = [[(axis, step) for axis in axes for step in _bits(lax.axis_size(axis), True)] for axes in axes_of]
    while any(plans):
        head = next(plan[0] for plan in plans if plan)
        which = [k for k, plan in enumerate(plans) if plan and plan[0] == head]
        axis, step = head
        count = lax.axis_size(axis)
        low = (lax.axis_index(axis) & step) == 0
        others = lax.ppermute([xs[k] for k in which], axis, [(i, i ^ step) for i in range(count)])
        for k, other in zip(which, others):
            xs[k] = jnp.where(low, jnp.concatenate([xs[k], other], 0), jnp.concatenate([other, xs[k]], 0))
            plans[k] = plans[k][1:]
    return xs


def _halving_sum(x, axis):
    count = lax.axis_size(axis)
    if count & (count - 1) or x.shape[0] % count:
        return _butterfly_sum(x, axis)
    here = lax.axis_index(axis)
    steps = _bits(count, False)
    for step in steps:
        half = x.shape[0] // 2
        low = (here & step) == 0
        keep = jnp.where(low, x[:half], x[half:])
        give = jnp.where(low, x[half:], x[:half])
        x = keep + lax.ppermute(give, axis, [(i, i ^ step) for i in range(count)])
    for step in steps[::-1]:
        low = (here & step) == 0
        other = lax.ppermute(x, axis, [(i, i ^ step) for i in range(count)])
        x = jnp.where(low, jnp.concatenate([x, other], 0), jnp.concatenate([other, x], 0))
    return x


def _qr_step(image, gram_axis):
    gram_part = jnp.dot(
        image.T, image, precision=lax.Precision.HIGHEST, preferred_element_type=jnp.float32
    )
    gram_matrix = _direct_sum(gram_part, gram_axis)
    lower_factor = jnp.linalg.cholesky(gram_matrix)
    inverse = jax.scipy.linalg.solve_triangular(
        lower_factor, jnp.eye(lower_factor.shape[0], dtype=lower_factor.dtype), lower=True
    )
    return lax.dot_general(
        image, inverse, (((1,), (1,)), ((), ())),
        precision=lax.Precision.HIGHEST, preferred_element_type=jnp.float32,
    )


def shards(snapshots, focus_in, focus_out, start_basis):
    rows_here, bins_here, snaps_here = snapshots.shape
    bin_count = lax.axis_size("bin")
    row_count = lax.axis_size("row")
    col_count = lax.axis_size("col")
    col_here = lax.axis_index("col")
    row_here = lax.axis_index("row")
    partial_proj = jnp.einsum(
        "mbs,bmr->brs", snapshots, focus_in, preferred_element_type=jnp.float32
    )
    projected = _direct_sum(partial_proj, "row").astype(jnp.bfloat16)
    lifted = jnp.einsum("bmr,brs->mbs", focus_out, projected, preferred_element_type=jnp.float32)
    focused = (snapshots.astype(jnp.float32) + lifted).astype(jnp.bfloat16)
    columns = bins_here * snaps_here
    local_rows = focused.reshape(rows_here, columns)
    array_size = rows_here * row_count
    col_block = array_size // col_count
    scaling = 1.0 / (columns * col_count * bin_count)

    power_of_two = all(n & (n - 1) == 0 for n in (bin_count, row_count, col_count))
    if row_count == col_count and power_of_two:
        swapped = lax.ppermute(local_rows, ("row", "col"), _transpose_pairs(row_count, col_count))
        swapped = jnp.where(row_here == col_here, local_rows, swapped)
        right_rows, left_rows = _butterfly_gather(
            [local_rows, swapped], [("bin", "col"), ("bin", "row")]
        )
    else:
        right_rows = lax.all_gather(local_rows, ("bin", "col"), axis=0, tiled=False)
        every_row = lax.all_gather(right_rows, "row", axis=1, tiled=True)
        left_rows = lax.dynamic_slice_in_dim(every_row, col_here * col_block, col_block, 1)
    covariance = lax.dot_general(
        left_rows, right_rows, (((0, 2), (0, 2)), ((), ())), preferred_element_type=jnp.float32
    ) * scaling

    basis_rows = lax.dynamic_slice_in_dim(start_basis, row_here * rows_here, rows_here, 0)
    on_rows = True
    for sweep_index in range(ITERS):
        if on_rows:
            partial_image = jnp.dot(
                covariance, basis_rows, precision=lax.Precision.HIGHEST,
                preferred_element_type=jnp.float32,
            )
            image = _butterfly_sum(partial_image, "row")
            basis_rows = _qr_step(image, "col")
        else:
            partial_image = lax.dot_general(
                covariance, basis_rows, (((0,), (0,)), ((), ())),
                precision=lax.Precision.HIGHEST, preferred_element_type=jnp.float32,
            )
            image = _halving_sum(partial_image, "col")
            basis_rows = _qr_step(image, "row")
        on_rows = not on_rows
    if not on_rows:
        swapped = lax.ppermute(basis_rows, ("row", "col"), _transpose_pairs(row_count, col_count))
        basis_rows = jnp.where(row_here == col_here, basis_rows, swapped)
    out_rows = array_size // (row_count * col_count)
    basis_out = lax.dynamic_slice_in_dim(basis_rows, col_here * out_rows, out_rows, 0) * math.sqrt(array_size)
    return (covariance, basis_out)


def solution(mesh):
    in_specs = (P("row", "bin", "col"), P("bin", "row", None), P("bin", "row", None), P())
    out_specs = (P("col", "row"), P(("row", "col"), None))
    return jax.shard_map(shards, mesh=mesh, in_specs=in_specs, out_specs=out_specs, check_vma=False)
```

```python
import math

import jax
import jax.numpy as jnp
from jax import lax
from jax.sharding import PartitionSpec as P

ITERS = 2


def _transpose_pairs(row_count, col_count):
    return [
        (i * col_count + j, j * row_count + i)
        for i in range(row_count)
        for j in range(col_count)
        if i != j
    ]


def _butterfly_sum(x, axis):
    count = lax.axis_size(axis)
    if count & (count - 1):
        return lax.psum(x, axis)
    step = 1
    while step < count:
        x = x + lax.ppermute(x, axis, [(i, i ^ step) for i in range(count)])
        step *= 2
    return x


def _bits(count, far_first):
    steps = []
    step = 1
    while step < count:
        steps.append(step)
        step *= 2
    return steps[::-1] if far_first else steps


def _direct_sum(x, axis):
    count = lax.axis_size(axis)
    if count != 4:
        return _butterfly_sum(x, axis)
    got = [lax.ppermute(x, axis, [(i, i ^ k) for i in range(count)]) for k in (1, 2, 3)]
    return (x + got[0]) + (got[1] + got[2])


def _butterfly_gather(xs, axes_of):
    xs = [x[None] for x in xs]
    plans = [[(axis, step) for axis in axes for step in _bits(lax.axis_size(axis), True)] for axes in axes_of]
    while any(plans):
        head = next(plan[0] for plan in plans if plan)
        which = [k for k, plan in enumerate(plans) if plan and plan[0] == head]
        axis, step = head
        count = lax.axis_size(axis)
        low = (lax.axis_index(axis) & step) == 0
        others = lax.ppermute([xs[k] for k in which], axis, [(i, i ^ step) for i in range(count)])
        for k, other in zip(which, others):
            xs[k] = jnp.where(low, jnp.concatenate([xs[k], other], 0), jnp.concatenate([other, xs[k]], 0))
            plans[k] = plans[k][1:]
    return xs


def _halving_sum(x, axis):
    count = lax.axis_size(axis)
    if count & (count - 1) or x.shape[0] % count:
        return _butterfly_sum(x, axis)
    here = lax.axis_index(axis)
    steps = _bits(count, False)
    for step in steps:
        half = x.shape[0] // 2
        low = (here & step) == 0
        keep = jnp.where(low, x[:half], x[half:])
        give = jnp.where(low, x[half:], x[:half])
        x = keep + lax.ppermute(give, axis, [(i, i ^ step) for i in range(count)])
    for step in steps[::-1]:
        low = (here & step) == 0
        other = lax.ppermute(x, axis, [(i, i ^ step) for i in range(count)])
        x = jnp.where(low, jnp.concatenate([x, other], 0), jnp.concatenate([other, x], 0))
    return x


def _lower_factor(image, gram_axis):
    gram_part = jnp.dot(
        image.T, image, precision=lax.Precision.HIGHEST, preferred_element_type=jnp.float32
    )
    return jnp.linalg.cholesky(_direct_sum(gram_part, gram_axis))


def _right_solve(lower_factor, image):
    return jax.scipy.linalg.solve_triangular(lower_factor, image.T, lower=True).T


def shards(snapshots, focus_in, focus_out, start_basis):
    rows_here, bins_here, snaps_here = snapshots.shape
    bin_count = lax.axis_size("bin")
    row_count = lax.axis_size("row")
    col_count = lax.axis_size("col")
    col_here = lax.axis_index("col")
    row_here = lax.axis_index("row")
    partial_proj = jnp.einsum(
        "mbs,bmr->brs", snapshots, focus_in, preferred_element_type=jnp.float32
    )
    projected = _direct_sum(partial_proj, "row").astype(jnp.bfloat16)
    lifted = jnp.einsum("bmr,brs->mbs", focus_out, projected, preferred_element_type=jnp.float32)
    focused = (snapshots.astype(jnp.float32) + lifted).astype(jnp.bfloat16)
    columns = bins_here * snaps_here
    local_rows = focused.reshape(rows_here, columns)
    array_size = rows_here * row_count
    col_block = array_size // col_count
    scaling = 1.0 / (columns * col_count * bin_count)

    power_of_two = all(n & (n - 1) == 0 for n in (bin_count, row_count, col_count))
    if row_count == col_count and power_of_two:
        swapped = lax.ppermute(local_rows, ("row", "col"), _transpose_pairs(row_count, col_count))
        swapped = jnp.where(row_here == col_here, local_rows, swapped)
        right_rows, left_rows = _butterfly_gather(
            [local_rows, swapped], [("bin", "col"), ("bin", "row")]
        )
    else:
        right_rows = lax.all_gather(local_rows, ("bin", "col"), axis=0, tiled=False)
        every_row = lax.all_gather(right_rows, "row", axis=1, tiled=True)
        left_rows = lax.dynamic_slice_in_dim(every_row, col_here * col_block, col_block, 1)
    covariance = lax.dot_general(
        left_rows, right_rows, (((0, 2), (0, 2)), ((), ())), preferred_element_type=jnp.float32
    ) * scaling

    def cov_times(block, on_rows):
        if on_rows:
            partial_image = jnp.dot(
                covariance, block, precision=lax.Precision.HIGHEST,
                preferred_element_type=jnp.float32,
            )
            return _butterfly_sum(partial_image, "row")
        partial_image = lax.dot_general(
            covariance, block, (((0,), (0,)), ((), ())),
            precision=lax.Precision.HIGHEST, preferred_element_type=jnp.float32,
        )
        return _halving_sum(partial_image, "col")

    basis_rows = lax.dynamic_slice_in_dim(start_basis, row_here * rows_here, rows_here, 0)
    image = cov_times(basis_rows, True)
    on_rows = False
    for sweep_index in range(ITERS):
        lower_factor = _lower_factor(image, "row" if on_rows else "col")
        if sweep_index == ITERS - 1:
            basis_rows = _right_solve(lower_factor, image)
            break
        image = _right_solve(lower_factor, cov_times(image, on_rows))
        on_rows = not on_rows
    if not on_rows:
        swapped = lax.ppermute(basis_rows, ("row", "col"), _transpose_pairs(row_count, col_count))
        basis_rows = jnp.where(row_here == col_here, basis_rows, swapped)
    out_rows = array_size // (row_count * col_count)
    basis_out = lax.dynamic_slice_in_dim(basis_rows, col_here * out_rows, out_rows, 0) * math.sqrt(array_size)
    return (covariance, basis_out)


def solution(mesh):
    in_specs = (P("row", "bin", "col"), P("bin", "row", None), P("bin", "row", None), P())
    out_specs = (P("col", "row"), P(("row", "col"), None))
    return jax.shard_map(shards, mesh=mesh, in_specs=in_specs, out_specs=out_specs, check_vma=False)
```

```python
import math

import jax
import jax.numpy as jnp
from jax import lax
from jax.sharding import PartitionSpec as P

ITERS = 2


def _transpose_pairs(row_count, col_count):
    return [
        (i * col_count + j, j * row_count + i)
        for i in range(row_count)
        for j in range(col_count)
        if i != j
    ]


def _butterfly_sum(x, axis):
    count = lax.axis_size(axis)
    if count & (count - 1):
        return lax.psum(x, axis)
    step = 1
    while step < count:
        x = x + lax.ppermute(x, axis, [(i, i ^ step) for i in range(count)])
        step *= 2
    return x


def _bits(count, far_first):
    steps = []
    step = 1
    while step < count:
        steps.append(step)
        step *= 2
    return steps[::-1] if far_first else steps


def _direct_sum(x, axis):
    count = lax.axis_size(axis)
    if count != 4:
        return _butterfly_sum(x, axis)
    got = [lax.ppermute(x, axis, [(i, i ^ k) for i in range(count)]) for k in (1, 2, 3)]
    return (x + got[0]) + (got[1] + got[2])


def _butterfly_gather(x, plan):
    x = x[None]
    for axis, step, slot in plan:
        count = lax.axis_size(axis)
        low = (lax.axis_index(axis) & step) == 0
        other = lax.ppermute(x, axis, [(i, i ^ step) for i in range(count)])
        below = 2 ** sum(1 for _, _, done in plan[: plan.index((axis, step, slot))] if done < slot)
        mine = x.reshape((-1, 1, below) + x.shape[1:])
        theirs = other.reshape(mine.shape)
        x = jnp.where(low, jnp.concatenate([mine, theirs], 1), jnp.concatenate([theirs, mine], 1))
        x = x.reshape((-1,) + x.shape[3:])
    return x


def _halving_sum(x, axis):
    count = lax.axis_size(axis)
    if count & (count - 1) or x.shape[0] % count:
        return _butterfly_sum(x, axis)
    here = lax.axis_index(axis)
    steps = _bits(count, False)
    for step in steps:
        half = x.shape[0] // 2
        low = (here & step) == 0
        keep = jnp.where(low, x[:half], x[half:])
        give = jnp.where(low, x[half:], x[:half])
        x = keep + lax.ppermute(give, axis, [(i, i ^ step) for i in range(count)])
    for step in steps[::-1]:
        low = (here & step) == 0
        other = lax.ppermute(x, axis, [(i, i ^ step) for i in range(count)])
        x = jnp.where(low, jnp.concatenate([x, other], 0), jnp.concatenate([other, x], 0))
    return x


def _lower_factor(image, gram_axis):
    gram_part = jnp.dot(
        image.T, image, precision=lax.Precision.HIGHEST, preferred_element_type=jnp.float32
    )
    return jnp.linalg.cholesky(_direct_sum(gram_part, gram_axis))


def _right_solve(lower_factor, image):
    return jax.scipy.linalg.solve_triangular(lower_factor, image.T, lower=True).T


def shards(snapshots, focus_in, focus_out, start_basis):
    rows_here, bins_here, snaps_here = snapshots.shape
    bin_count = lax.axis_size("bin")
    row_count = lax.axis_size("row")
    col_count = lax.axis_size("col")
    col_here = lax.axis_index("col")
    row_here = lax.axis_index("row")
    partial_proj = jnp.einsum(
        "mbs,bmr->brs", snapshots, focus_in, preferred_element_type=jnp.float32
    )
    projected = _direct_sum(partial_proj, "row").astype(jnp.bfloat16)
    lifted = jnp.einsum("bmr,brs->mbs", focus_out, projected, preferred_element_type=jnp.float32)
    focused = (snapshots.astype(jnp.float32) + lifted).astype(jnp.bfloat16)
    columns = bins_here * snaps_here
    local_rows = focused.reshape(rows_here, columns)
    array_size = rows_here * row_count
    col_block = array_size // col_count
    scaling = 1.0 / (columns * col_count * bin_count)

    power_of_two = all(n & (n - 1) == 0 for n in (bin_count, row_count, col_count))
    if row_count == col_count and power_of_two:
        swapped = lax.ppermute(local_rows, ("row", "col"), _transpose_pairs(row_count, col_count))
        swapped = jnp.where(row_here == col_here, local_rows, swapped)
        group = _bits(col_count, True)
        bins = _bits(bin_count, True)
        right_plan = [("col", step, k) for k, step in enumerate(group)]
        right_plan += [("bin", step, len(group) + k) for k, step in enumerate(bins)]
        left_plan = [("bin", step, len(group) + k) for k, step in enumerate(bins)]
        left_plan += [("row", step, k) for k, step in enumerate(group)]
        right_rows = _butterfly_gather(local_rows, right_plan)
        left_rows = _butterfly_gather(swapped, left_plan)
    else:
        right_rows = lax.all_gather(local_rows, ("bin", "col"), axis=0, tiled=False)
        every_row = lax.all_gather(right_rows, "row", axis=1, tiled=True)
        left_rows = lax.dynamic_slice_in_dim(every_row, col_here * col_block, col_block, 1)
    covariance = lax.dot_general(
        left_rows, right_rows, (((0, 2), (0, 2)), ((), ())), preferred_element_type=jnp.float32
    ) * scaling

    def cov_times(block, on_rows):
        if on_rows:
            partial_image = jnp.dot(
                covariance, block, precision=lax.Precision.HIGHEST,
                preferred_element_type=jnp.float32,
            )
            return _butterfly_sum(partial_image, "row")
        partial_image = lax.dot_general(
            covariance, block, (((0,), (0,)), ((), ())),
            precision=lax.Precision.HIGHEST, preferred_element_type=jnp.float32,
        )
        return _halving_sum(partial_image, "col")

    basis_rows = lax.dynamic_slice_in_dim(start_basis, row_here * rows_here, rows_here, 0)
    image = cov_times(basis_rows, True)
    on_rows = False
    for sweep_index in range(ITERS):
        lower_factor = _lower_factor(image, "row" if on_rows else "col")
        if sweep_index == ITERS - 1:
            basis_rows = _right_solve(lower_factor, image)
            break
        image = _right_solve(lower_factor, cov_times(image, on_rows))
        on_rows = not on_rows
    if not on_rows:
        swapped = lax.ppermute(basis_rows, ("row", "col"), _transpose_pairs(row_count, col_count))
        basis_rows = jnp.where(row_here == col_here, basis_rows, swapped)
    out_rows = array_size // (row_count * col_count)
    basis_out = lax.dynamic_slice_in_dim(basis_rows, col_here * out_rows, out_rows, 0) * math.sqrt(array_size)
    return (covariance, basis_out)


def solution(mesh):
    in_specs = (P("row", "bin", "col"), P("bin", "row", None), P("bin", "row", None), P())
    out_specs = (P("col", "row"), P(("row", "col"), None))
    return jax.shard_map(shards, mesh=mesh, in_specs=in_specs, out_specs=out_specs, check_vma=False)
```

```python
import math

import jax
import jax.numpy as jnp
from jax import lax
from jax.sharding import PartitionSpec as P

ITERS = 2


def _transpose_pairs(row_count, col_count):
    return [
        (i * col_count + j, j * row_count + i)
        for i in range(row_count)
        for j in range(col_count)
        if i != j
    ]


def _butterfly_sum(x, axis):
    count = lax.axis_size(axis)
    if count & (count - 1):
        return lax.psum(x, axis)
    step = 1
    while step < count:
        x = x + lax.ppermute(x, axis, [(i, i ^ step) for i in range(count)])
        step *= 2
    return x


def _bits(count, far_first):
    steps = []
    step = 1
    while step < count:
        steps.append(step)
        step *= 2
    return steps[::-1] if far_first else steps


def _direct_sum(x, axis):
    count = lax.axis_size(axis)
    if count != 4:
        return _butterfly_sum(x, axis)
    got = [lax.ppermute(x, axis, [(i, i ^ k) for i in range(count)]) for k in (1, 2, 3)]
    return (x + got[0]) + (got[1] + got[2])


def _butterfly_gather(x, plan):
    x = x[None]
    for axis, step, slot in plan:
        count = lax.axis_size(axis)
        low = (lax.axis_index(axis) & step) == 0
        other = lax.ppermute(x, axis, [(i, i ^ step) for i in range(count)])
        below = 2 ** sum(1 for _, _, done in plan[: plan.index((axis, step, slot))] if done < slot)
        mine = x.reshape((-1, 1, below) + x.shape[1:])
        theirs = other.reshape(mine.shape)
        first = jnp.where(low, 0, 1)
        both = jnp.zeros((mine.shape[0], 2) + mine.shape[2:], x.dtype)
        both = lax.dynamic_update_slice_in_dim(both, mine, first, 1)
        both = lax.dynamic_update_slice_in_dim(both, theirs, 1 - first, 1)
        x = both.reshape((-1,) + x.shape[1:])
    return x


def _halving_sum(x, axis):
    count = lax.axis_size(axis)
    if count & (count - 1) or x.shape[0] % count:
        return _butterfly_sum(x, axis)
    here = lax.axis_index(axis)
    steps = _bits(count, False)
    for step in steps:
        half = x.shape[0] // 2
        low = (here & step) == 0
        keep = jnp.where(low, x[:half], x[half:])
        give = jnp.where(low, x[half:], x[:half])
        x = keep + lax.ppermute(give, axis, [(i, i ^ step) for i in range(count)])
    for step in steps[::-1]:
        low = (here & step) == 0
        other = lax.ppermute(x, axis, [(i, i ^ step) for i in range(count)])
        first = jnp.where(low, 0, x.shape[0])
        both = jnp.zeros((2 * x.shape[0],) + x.shape[1:], x.dtype)
        both = lax.dynamic_update_slice_in_dim(both, x, first, 0)
        x = lax.dynamic_update_slice_in_dim(both, other, x.shape[0] - first, 0)
    return x


def _lower_factor(image, gram_axis):
    gram_part = jnp.dot(
        image.T, image, precision=lax.Precision.HIGHEST, preferred_element_type=jnp.float32
    )
    return jnp.linalg.cholesky(_direct_sum(gram_part, gram_axis))


def _right_solve(lower_factor, image):
    return jax.scipy.linalg.solve_triangular(lower_factor, image.T, lower=True).T


def shards(snapshots, focus_in, focus_out, start_basis):
    rows_here, bins_here, snaps_here = snapshots.shape
    bin_count = lax.axis_size("bin")
    row_count = lax.axis_size("row")
    col_count = lax.axis_size("col")
    col_here = lax.axis_index("col")
    row_here = lax.axis_index("row")
    partial_proj = jnp.einsum(
        "mbs,bmr->brs", snapshots, focus_in, preferred_element_type=jnp.float32
    )
    projected = _direct_sum(partial_proj, "row").astype(jnp.bfloat16)
    lifted = jnp.einsum("bmr,brs->mbs", focus_out, projected, preferred_element_type=jnp.float32)
    focused = (snapshots.astype(jnp.float32) + lifted).astype(jnp.bfloat16)
    columns = bins_here * snaps_here
    local_rows = focused.reshape(rows_here, columns)
    array_size = rows_here * row_count
    col_block = array_size // col_count
    scaling = 1.0 / (columns * col_count * bin_count)

    power_of_two = all(n & (n - 1) == 0 for n in (bin_count, row_count, col_count))
    if row_count == col_count and power_of_two:
        swapped = lax.ppermute(local_rows, ("row", "col"), _transpose_pairs(row_count, col_count))
        swapped = jnp.where(row_here == col_here, local_rows, swapped)
        group = _bits(col_count, True)
        bins = _bits(bin_count, True)
        right_plan = [("col", step, k) for k, step in enumerate(group)]
        right_plan += [("bin", step, len(group) + k) for k, step in enumerate(bins)]
        left_plan = [("bin", step, len(group) + k) for k, step in enumerate(bins)]
        left_plan += [("row", step, k) for k, step in enumerate(group)]
        right_rows = _butterfly_gather(local_rows, right_plan)
        left_rows = _butterfly_gather(swapped, left_plan)
    else:
        right_rows = lax.all_gather(local_rows, ("bin", "col"), axis=0, tiled=False)
        every_row = lax.all_gather(right_rows, "row", axis=1, tiled=True)
        left_rows = lax.dynamic_slice_in_dim(every_row, col_here * col_block, col_block, 1)
    covariance = lax.dot_general(
        left_rows, right_rows, (((0, 2), (0, 2)), ((), ())), preferred_element_type=jnp.float32
    ) * scaling

    def cov_times(block, on_rows):
        if on_rows:
            partial_image = jnp.dot(
                covariance, block, precision=lax.Precision.HIGHEST,
                preferred_element_type=jnp.float32,
            )
            return _halving_sum(partial_image, "row")
        partial_image = lax.dot_general(
            covariance, block, (((0,), (0,)), ((), ())),
            precision=lax.Precision.HIGHEST, preferred_element_type=jnp.float32,
        )
        return _halving_sum(partial_image, "col")

    basis_rows = lax.dynamic_slice_in_dim(start_basis, row_here * rows_here, rows_here, 0)
    image = cov_times(basis_rows, True)
    on_rows = False
    for sweep_index in range(ITERS):
        lower_factor = _lower_factor(image, "row" if on_rows else "col")
        if sweep_index == ITERS - 1:
            basis_rows = _right_solve(lower_factor, image)
            break
        image = _right_solve(lower_factor, cov_times(image, on_rows))
        on_rows = not on_rows
    if not on_rows:
        swapped = lax.ppermute(basis_rows, ("row", "col"), _transpose_pairs(row_count, col_count))
        basis_rows = jnp.where(row_here == col_here, basis_rows, swapped)
    out_rows = array_size // (row_count * col_count)
    basis_out = lax.dynamic_slice_in_dim(basis_rows, col_here * out_rows, out_rows, 0) * math.sqrt(array_size)
    return (covariance, basis_out)


def solution(mesh):
    in_specs = (P("row", "bin", "col"), P("bin", "row", None), P("bin", "row", None), P())
    out_specs = (P("col", "row"), P(("row", "col"), None))
    return jax.shard_map(shards, mesh=mesh, in_specs=in_specs, out_specs=out_specs, check_vma=False)
```

```python
import math

import jax
import jax.numpy as jnp
from jax import lax
from jax.sharding import PartitionSpec as P

ITERS = 2


def _transpose_pairs(row_count, col_count):
    return [
        (i * col_count + j, j * row_count + i)
        for i in range(row_count)
        for j in range(col_count)
        if i != j
    ]


def _butterfly_sum(x, axis):
    count = lax.axis_size(axis)
    if count & (count - 1):
        return lax.psum(x, axis)
    step = 1
    while step < count:
        x = x + lax.ppermute(x, axis, [(i, i ^ step) for i in range(count)])
        step *= 2
    return x


def _bits(count, far_first):
    steps = []
    step = 1
    while step < count:
        steps.append(step)
        step *= 2
    return steps[::-1] if far_first else steps


def _direct_sum(x, axis):
    count = lax.axis_size(axis)
    if count != 4:
        return _butterfly_sum(x, axis)
    got = [lax.ppermute(x, axis, [(i, i ^ k) for i in range(count)]) for k in (1, 2, 3)]
    return (x + got[0]) + (got[1] + got[2])


def _butterfly_gather(x, plan):
    x = x[None]
    for axis, step, slot in plan:
        count = lax.axis_size(axis)
        low = (lax.axis_index(axis) & step) == 0
        other = lax.ppermute(x, axis, [(i, i ^ step) for i in range(count)])
        below = 2 ** sum(1 for _, _, done in plan[: plan.index((axis, step, slot))] if done < slot)
        mine = x.reshape((-1, 1, below) + x.shape[1:])
        theirs = other.reshape(mine.shape)
        first = jnp.where(low, 0, 1)
        both = jnp.zeros((mine.shape[0], 2) + mine.shape[2:], x.dtype)
        both = lax.dynamic_update_slice_in_dim(both, mine, first, 1)
        both = lax.dynamic_update_slice_in_dim(both, theirs, 1 - first, 1)
        x = both.reshape((-1,) + x.shape[1:])
    return x


def _halving_sum(x, axis):
    count = lax.axis_size(axis)
    if count & (count - 1) or x.shape[0] % count:
        return _butterfly_sum(x, axis)
    here = lax.axis_index(axis)
    steps = _bits(count, False)
    for step in steps:
        half = x.shape[0] // 2
        low = (here & step) == 0
        keep = jnp.where(low, x[:half], x[half:])
        give = jnp.where(low, x[half:], x[:half])
        x = keep + lax.ppermute(give, axis, [(i, i ^ step) for i in range(count)])
    for step in steps[::-1]:
        low = (here & step) == 0
        other = lax.ppermute(x, axis, [(i, i ^ step) for i in range(count)])
        first = jnp.where(low, 0, x.shape[0])
        both = jnp.zeros((2 * x.shape[0],) + x.shape[1:], x.dtype)
        both = lax.dynamic_update_slice_in_dim(both, x, first, 0)
        x = lax.dynamic_update_slice_in_dim(both, other, x.shape[0] - first, 0)
    return x


def _lower_factor(image, gram_axis):
    gram_part = jnp.dot(
        image.T, image, precision=lax.Precision.HIGHEST, preferred_element_type=jnp.float32
    )
    return jnp.linalg.cholesky(_direct_sum(gram_part, gram_axis))


def _right_solve(lower_factor, image):
    return jax.scipy.linalg.solve_triangular(lower_factor, image.T, lower=True).T


def shards(snapshots, focus_in, focus_out, start_basis):
    rows_here, bins_here, snaps_here = snapshots.shape
    bin_count = lax.axis_size("bin")
    row_count = lax.axis_size("row")
    col_count = lax.axis_size("col")
    col_here = lax.axis_index("col")
    row_here = lax.axis_index("row")
    partial_proj = jnp.einsum(
        "mbs,bmr->brs", snapshots, focus_in, preferred_element_type=jnp.float32
    )
    projected = _direct_sum(partial_proj, "row").astype(jnp.bfloat16)
    lifted = jnp.einsum("bmr,brs->mbs", focus_out, projected, preferred_element_type=jnp.float32)
    focused = (snapshots.astype(jnp.float32) + lifted).astype(jnp.bfloat16)
    columns = bins_here * snaps_here
    local_rows = focused.reshape(rows_here, columns)
    array_size = rows_here * row_count
    col_block = array_size // col_count
    scaling = 1.0 / (columns * col_count * bin_count)

    power_of_two = all(n & (n - 1) == 0 for n in (bin_count, row_count, col_count))
    if row_count == col_count and power_of_two:
        swapped = lax.ppermute(local_rows, ("row", "col"), _transpose_pairs(row_count, col_count))
        swapped = jnp.where(row_here == col_here, local_rows, swapped)
        group = _bits(col_count, True)
        bins = _bits(bin_count, True)
        right_plan = [("col", step, k) for k, step in enumerate(group)]
        right_plan += [("bin", step, len(group) + k) for k, step in enumerate(bins)]
        left_plan = [("bin", step, len(group) + k) for k, step in enumerate(bins)]
        left_plan += [("row", step, k) for k, step in enumerate(group)]
        half = rows_here // 2
        early_bin = [step for step in right_plan if step[0] == "bin"]
        early_bin += [step for step in right_plan if step[0] != "bin"]
        right_rows = jnp.concatenate(
            [
                _butterfly_gather(local_rows[:half], right_plan),
                _butterfly_gather(local_rows[half:], early_bin),
            ],
            1,
        )
        left_rows = _butterfly_gather(swapped, left_plan)
    else:
        right_rows = lax.all_gather(local_rows, ("bin", "col"), axis=0, tiled=False)
        every_row = lax.all_gather(right_rows, "row", axis=1, tiled=True)
        left_rows = lax.dynamic_slice_in_dim(every_row, col_here * col_block, col_block, 1)
    covariance = lax.dot_general(
        left_rows, right_rows, (((0, 2), (0, 2)), ((), ())), preferred_element_type=jnp.float32
    ) * scaling

    def cov_times(block, on_rows):
        if on_rows:
            partial_image = jnp.dot(
                covariance, block, precision=lax.Precision.HIGHEST,
                preferred_element_type=jnp.float32,
            )
            return _butterfly_sum(partial_image, "row")
        partial_image = lax.dot_general(
            covariance, block, (((0,), (0,)), ((), ())),
            precision=lax.Precision.HIGHEST, preferred_element_type=jnp.float32,
        )
        return _halving_sum(partial_image, "col")

    basis_rows = lax.dynamic_slice_in_dim(start_basis, row_here * rows_here, rows_here, 0)
    image = cov_times(basis_rows, True)
    on_rows = False
    for sweep_index in range(ITERS):
        lower_factor = _lower_factor(image, "row" if on_rows else "col")
        if sweep_index == ITERS - 1:
            basis_rows = _right_solve(lower_factor, image)
            break
        image = _right_solve(lower_factor, cov_times(image, on_rows))
        on_rows = not on_rows
    if not on_rows:
        swapped = lax.ppermute(basis_rows, ("row", "col"), _transpose_pairs(row_count, col_count))
        basis_rows = jnp.where(row_here == col_here, basis_rows, swapped)
    out_rows = array_size // (row_count * col_count)
    basis_out = lax.dynamic_slice_in_dim(basis_rows, col_here * out_rows, out_rows, 0) * math.sqrt(array_size)
    return (covariance, basis_out)


def solution(mesh):
    in_specs = (P("row", "bin", "col"), P("bin", "row", None), P("bin", "row", None), P())
    out_specs = (P("col", "row"), P(("row", "col"), None))
    return jax.shard_map(shards, mesh=mesh, in_specs=in_specs, out_specs=out_specs, check_vma=False)
```

```python
import math

import jax
import jax.numpy as jnp
from jax import lax
from jax.sharding import PartitionSpec as P

ITERS = 2


def _transpose_pairs(row_count, col_count):
    return [
        (i * col_count + j, j * row_count + i)
        for i in range(row_count)
        for j in range(col_count)
        if i != j
    ]


def _butterfly_sum(x, axis):
    count = lax.axis_size(axis)
    if count & (count - 1):
        return lax.psum(x, axis)
    step = 1
    while step < count:
        x = x + lax.ppermute(x, axis, [(i, i ^ step) for i in range(count)])
        step *= 2
    return x


def _bits(count, far_first):
    steps = []
    step = 1
    while step < count:
        steps.append(step)
        step *= 2
    return steps[::-1] if far_first else steps


def _direct_sum(x, axis):
    count = lax.axis_size(axis)
    if count != 4:
        return _butterfly_sum(x, axis)
    got = [lax.ppermute(x, axis, [(i, i ^ k) for i in range(count)]) for k in (1, 2, 3)]
    return (x + got[0]) + (got[1] + got[2])


def _butterfly_gather(x, plan):
    x = x[None]
    for axis, step, slot in plan:
        count = lax.axis_size(axis)
        low = (lax.axis_index(axis) & step) == 0
        other = lax.ppermute(x, axis, [(i, i ^ step) for i in range(count)])
        below = 2 ** sum(1 for _, _, done in plan[: plan.index((axis, step, slot))] if done < slot)
        mine = x.reshape((-1, 1, below) + x.shape[1:])
        theirs = other.reshape(mine.shape)
        first = jnp.where(low, 0, 1)
        both = jnp.zeros((mine.shape[0], 2) + mine.shape[2:], x.dtype)
        both = lax.dynamic_update_slice_in_dim(both, mine, first, 1)
        both = lax.dynamic_update_slice_in_dim(both, theirs, 1 - first, 1)
        x = both.reshape((-1,) + x.shape[1:])
    return x


def _halving_sum(x, axis):
    count = lax.axis_size(axis)
    if count & (count - 1) or x.shape[0] % count:
        return _butterfly_sum(x, axis)
    here = lax.axis_index(axis)
    steps = _bits(count, False)
    for step in steps:
        half = x.shape[0] // 2
        low = (here & step) == 0
        keep = jnp.where(low, x[:half], x[half:])
        give = jnp.where(low, x[half:], x[:half])
        x = keep + lax.ppermute(give, axis, [(i, i ^ step) for i in range(count)])
    for step in steps[::-1]:
        low = (here & step) == 0
        other = lax.ppermute(x, axis, [(i, i ^ step) for i in range(count)])
        first = jnp.where(low, 0, x.shape[0])
        both = jnp.zeros((2 * x.shape[0],) + x.shape[1:], x.dtype)
        both = lax.dynamic_update_slice_in_dim(both, x, first, 0)
        x = lax.dynamic_update_slice_in_dim(both, other, x.shape[0] - first, 0)
    return x


def _pair_split_sum(x, axis):
    count = lax.axis_size(axis)
    if count != 4 or x.shape[0] % 2:
        return _butterfly_sum(x, axis)
    pairs = [(i, i ^ 1) for i in range(count)]
    near_low = (lax.axis_index(axis) & 1) == 0
    x = x + lax.ppermute(x, axis, pairs)
    half = x.shape[0] // 2
    mine = jnp.where(near_low, x[:half], x[half:])
    mine = mine + lax.ppermute(mine, axis, [(i, i ^ 2) for i in range(count)])
    other = lax.ppermute(mine, axis, pairs)
    first = jnp.where(near_low, 0, half)
    both = jnp.zeros(x.shape, x.dtype)
    both = lax.dynamic_update_slice_in_dim(both, mine, first, 0)
    return lax.dynamic_update_slice_in_dim(both, other, half - first, 0)


def _lower_factor(image, gram_axis):
    gram_part = jnp.dot(
        image.T, image, precision=lax.Precision.HIGHEST, preferred_element_type=jnp.float32
    )
    return jnp.linalg.cholesky(_direct_sum(gram_part, gram_axis))


def _right_solve(lower_factor, image):
    return jax.scipy.linalg.solve_triangular(lower_factor, image.T, lower=True).T


def shards(snapshots, focus_in, focus_out, start_basis):
    rows_here, bins_here, snaps_here = snapshots.shape
    bin_count = lax.axis_size("bin")
    row_count = lax.axis_size("row")
    col_count = lax.axis_size("col")
    col_here = lax.axis_index("col")
    row_here = lax.axis_index("row")
    partial_proj = jnp.einsum(
        "mbs,bmr->brs", snapshots, focus_in, preferred_element_type=jnp.float32
    )
    projected = _direct_sum(partial_proj, "row").astype(jnp.bfloat16)
    lifted = jnp.einsum("bmr,brs->mbs", focus_out, projected, preferred_element_type=jnp.float32)
    focused = (snapshots.astype(jnp.float32) + lifted).astype(jnp.bfloat16)
    columns = bins_here * snaps_here
    local_rows = focused.reshape(rows_here, columns)
    array_size = rows_here * row_count
    col_block = array_size // col_count
    scaling = 1.0 / (columns * col_count * bin_count)

    power_of_two = all(n & (n - 1) == 0 for n in (bin_count, row_count, col_count))
    if row_count == col_count and power_of_two:
        swapped = lax.ppermute(local_rows, ("row", "col"), _transpose_pairs(row_count, col_count))
        swapped = jnp.where(row_here == col_here, local_rows, swapped)
        group = _bits(col_count, True)
        bins = _bits(bin_count, True)
        right_plan = [("col", step, k) for k, step in enumerate(group)]
        right_plan += [("bin", step, len(group) + k) for k, step in enumerate(bins)]
        left_plan = [("bin", step, len(group) + k) for k, step in enumerate(bins)]
        left_plan += [("row", step, k) for k, step in enumerate(group)]
        half = rows_here // 2
        early_bin = [step for step in right_plan if step[0] == "bin"]
        early_bin += [step for step in right_plan if step[0] != "bin"]
        right_rows = jnp.concatenate(
            [
                _butterfly_gather(local_rows[:half], right_plan),
                _butterfly_gather(local_rows[half:], early_bin),
            ],
            1,
        )
        left_rows = _butterfly_gather(swapped, left_plan)
    else:
        right_rows = lax.all_gather(local_rows, ("bin", "col"), axis=0, tiled=False)
        every_row = lax.all_gather(right_rows, "row", axis=1, tiled=True)
        left_rows = lax.dynamic_slice_in_dim(every_row, col_here * col_block, col_block, 1)
    covariance = lax.dot_general(
        left_rows, right_rows, (((0, 2), (0, 2)), ((), ())), preferred_element_type=jnp.float32
    ) * scaling

    def cov_times(block, on_rows):
        if on_rows:
            partial_image = jnp.dot(
                covariance, block, precision=lax.Precision.HIGHEST,
                preferred_element_type=jnp.float32,
            )
            return _pair_split_sum(partial_image, "row")
        partial_image = lax.dot_general(
            covariance, block, (((0,), (0,)), ((), ())),
            precision=lax.Precision.HIGHEST, preferred_element_type=jnp.float32,
        )
        return _halving_sum(partial_image, "col")

    basis_rows = lax.dynamic_slice_in_dim(start_basis, row_here * rows_here, rows_here, 0)
    image = cov_times(basis_rows, True)
    on_rows = False
    for sweep_index in range(ITERS):
        lower_factor = _lower_factor(image, "row" if on_rows else "col")
        if sweep_index == ITERS - 1:
            basis_rows = _right_solve(lower_factor, image)
            break
        image = _right_solve(lower_factor, cov_times(image, on_rows))
        on_rows = not on_rows
    if not on_rows:
        swapped = lax.ppermute(basis_rows, ("row", "col"), _transpose_pairs(row_count, col_count))
        basis_rows = jnp.where(row_here == col_here, basis_rows, swapped)
    out_rows = array_size // (row_count * col_count)
    basis_out = lax.dynamic_slice_in_dim(basis_rows, col_here * out_rows, out_rows, 0) * math.sqrt(array_size)
    return (covariance, basis_out)


def solution(mesh):
    in_specs = (P("row", "bin", "col"), P("bin", "row", None), P("bin", "row", None), P())
    out_specs = (P("col", "row"), P(("row", "col"), None))
    return jax.shard_map(shards, mesh=mesh, in_specs=in_specs, out_specs=out_specs, check_vma=False)
```

```python
import math

import jax
import jax.numpy as jnp
from jax import lax
from jax.sharding import PartitionSpec as P

ITERS = 2


def _transpose_pairs(row_count, col_count):
    return [
        (i * col_count + j, j * row_count + i)
        for i in range(row_count)
        for j in range(col_count)
        if i != j
    ]


def _butterfly_sum(x, axis):
    count = lax.axis_size(axis)
    if count & (count - 1):
        return lax.psum(x, axis)
    step = 1
    while step < count:
        x = x + lax.ppermute(x, axis, [(i, i ^ step) for i in range(count)])
        step *= 2
    return x


def _bits(count, far_first):
    steps = []
    step = 1
    while step < count:
        steps.append(step)
        step *= 2
    return steps[::-1] if far_first else steps


def _direct_sum(x, axis):
    count = lax.axis_size(axis)
    if count != 4:
        return _butterfly_sum(x, axis)
    got = [lax.ppermute(x, axis, [(i, i ^ k) for i in range(count)]) for k in (1, 2, 3)]
    return (x + got[0]) + (got[1] + got[2])


def _butterfly_gather(x, plan):
    x = x[None]
    for axis, step, slot in plan:
        count = lax.axis_size(axis)
        low = (lax.axis_index(axis) & step) == 0
        other = lax.ppermute(x, axis, [(i, i ^ step) for i in range(count)])
        below = 2 ** sum(1 for _, _, done in plan[: plan.index((axis, step, slot))] if done < slot)
        mine = x.reshape((-1, 1, below) + x.shape[1:])
        theirs = other.reshape(mine.shape)
        first = jnp.where(low, 0, 1)
        both = jnp.zeros((mine.shape[0], 2) + mine.shape[2:], x.dtype)
        both = lax.dynamic_update_slice_in_dim(both, mine, first, 1)
        both = lax.dynamic_update_slice_in_dim(both, theirs, 1 - first, 1)
        x = both.reshape((-1,) + x.shape[1:])
    return x


def _halving_sum(x, axis):
    count = lax.axis_size(axis)
    if count & (count - 1) or x.shape[0] % count:
        return _butterfly_sum(x, axis)
    here = lax.axis_index(axis)
    steps = _bits(count, False)
    for step in steps:
        half = x.shape[0] // 2
        low = (here & step) == 0
        keep = jnp.where(low, x[:half], x[half:])
        give = jnp.where(low, x[half:], x[:half])
        x = keep + lax.ppermute(give, axis, [(i, i ^ step) for i in range(count)])
    for step in steps[::-1]:
        low = (here & step) == 0
        other = lax.ppermute(x, axis, [(i, i ^ step) for i in range(count)])
        first = jnp.where(low, 0, x.shape[0])
        both = jnp.zeros((2 * x.shape[0],) + x.shape[1:], x.dtype)
        both = lax.dynamic_update_slice_in_dim(both, x, first, 0)
        x = lax.dynamic_update_slice_in_dim(both, other, x.shape[0] - first, 0)
    return x


def _pair_split_sum(x, axis):
    count = lax.axis_size(axis)
    if count != 4 or x.shape[0] % 2:
        return _butterfly_sum(x, axis)
    pairs = [(i, i ^ 1) for i in range(count)]
    near_low = (lax.axis_index(axis) & 1) == 0
    x = x + lax.ppermute(x, axis, pairs)
    half = x.shape[0] // 2
    mine = jnp.where(near_low, x[:half], x[half:])
    mine = mine + lax.ppermute(mine, axis, [(i, i ^ 2) for i in range(count)])
    other = lax.ppermute(mine, axis, pairs)
    first = jnp.where(near_low, 0, half)
    both = jnp.zeros(x.shape, x.dtype)
    both = lax.dynamic_update_slice_in_dim(both, mine, first, 0)
    return lax.dynamic_update_slice_in_dim(both, other, half - first, 0)


def _lower_factor(image, gram_axis):
    gram_part = jnp.dot(
        image.T, image, precision=lax.Precision.HIGHEST, preferred_element_type=jnp.float32
    )
    return jnp.linalg.cholesky(_direct_sum(gram_part, gram_axis))


def _right_solve(lower_factor, image):
    return jax.scipy.linalg.solve_triangular(lower_factor, image.T, lower=True).T


def shards(snapshots, focus_in, focus_out, start_basis):
    rows_here, bins_here, snaps_here = snapshots.shape
    bin_count = lax.axis_size("bin")
    row_count = lax.axis_size("row")
    col_count = lax.axis_size("col")
    col_here = lax.axis_index("col")
    row_here = lax.axis_index("row")
    partial_proj = jnp.einsum(
        "mbs,bmr->brs", snapshots, focus_in, preferred_element_type=jnp.float32
    )
    projected = _direct_sum(partial_proj, "row").astype(jnp.bfloat16)
    lifted = jnp.einsum("bmr,brs->mbs", focus_out, projected, preferred_element_type=jnp.float32)
    focused = (snapshots.astype(jnp.float32) + lifted).astype(jnp.bfloat16)
    columns = bins_here * snaps_here
    local_rows = focused.reshape(rows_here, columns)
    array_size = rows_here * row_count
    col_block = array_size // col_count
    scaling = 1.0 / (columns * col_count * bin_count)

    power_of_two = all(n & (n - 1) == 0 for n in (bin_count, row_count, col_count))
    if row_count == col_count and power_of_two:
        swapped = lax.ppermute(local_rows, ("row", "col"), _transpose_pairs(row_count, col_count))
        swapped = jnp.where(row_here == col_here, local_rows, swapped)
        group = _bits(col_count, True)
        bins = _bits(bin_count, True)
        right_plan = [("col", step, k) for k, step in enumerate(group)]
        right_plan += [("bin", step, len(group) + k) for k, step in enumerate(bins)]
        left_plan = [("bin", step, len(group) + k) for k, step in enumerate(bins)]
        left_plan += [("row", step, k) for k, step in enumerate(group)]
        half = rows_here // 2
        early_bin = [step for step in right_plan if step[0] == "bin"]
        early_bin += [step for step in right_plan if step[0] != "bin"]
        right_rows = jnp.concatenate(
            [
                _butterfly_gather(local_rows[:half], right_plan),
                _butterfly_gather(local_rows[half:], early_bin),
            ],
            1,
        )
        left_rows = _butterfly_gather(swapped, left_plan)
    else:
        right_rows = lax.all_gather(local_rows, ("bin", "col"), axis=0, tiled=False)
        every_row = lax.all_gather(right_rows, "row", axis=1, tiled=True)
        left_rows = lax.dynamic_slice_in_dim(every_row, col_here * col_block, col_block, 1)
    covariance = lax.dot_general(
        left_rows, right_rows, (((0, 2), (0, 2)), ((), ())), preferred_element_type=jnp.float32
    ) * scaling
    covariance_t = lax.dot_general(
        right_rows, left_rows, (((0, 2), (0, 2)), ((), ())), preferred_element_type=jnp.float32
    ) * scaling

    def cov_times(block, on_rows):
        if on_rows:
            partial_image = jnp.dot(
                covariance, block, precision=lax.Precision.HIGHEST,
                preferred_element_type=jnp.float32,
            )
            return _pair_split_sum(partial_image, "row")
        partial_image = jnp.dot(
            covariance_t, block, precision=lax.Precision.HIGHEST,
            preferred_element_type=jnp.float32,
        )
        return _halving_sum(partial_image, "col")

    basis_rows = lax.dynamic_slice_in_dim(start_basis, row_here * rows_here, rows_here, 0)
    image = cov_times(basis_rows, True)
    on_rows = False
    for sweep_index in range(ITERS):
        lower_factor = _lower_factor(image, "row" if on_rows else "col")
        if sweep_index == ITERS - 1:
            basis_rows = _right_solve(lower_factor, image)
            break
        image = _right_solve(lower_factor, cov_times(image, on_rows))
        on_rows = not on_rows
    if not on_rows:
        swapped = lax.ppermute(basis_rows, ("row", "col"), _transpose_pairs(row_count, col_count))
        basis_rows = jnp.where(row_here == col_here, basis_rows, swapped)
    out_rows = array_size // (row_count * col_count)
    basis_out = lax.dynamic_slice_in_dim(basis_rows, col_here * out_rows, out_rows, 0) * math.sqrt(array_size)
    return (covariance, basis_out)


def solution(mesh):
    in_specs = (P("row", "bin", "col"), P("bin", "row", None), P("bin", "row", None), P())
    out_specs = (P("col", "row"), P(("row", "col"), None))
    return jax.shard_map(shards, mesh=mesh, in_specs=in_specs, out_specs=out_specs, check_vma=False)
```

```python
import math

import jax
import jax.numpy as jnp
from jax import lax
from jax.sharding import PartitionSpec as P

ITERS = 2


def _transpose_pairs(row_count, col_count):
    return [
        (i * col_count + j, j * row_count + i)
        for i in range(row_count)
        for j in range(col_count)
        if i != j
    ]


def _butterfly_sum(x, axis):
    count = lax.axis_size(axis)
    if count & (count - 1):
        return lax.psum(x, axis)
    step = 1
    while step < count:
        x = x + lax.ppermute(x, axis, [(i, i ^ step) for i in range(count)])
        step *= 2
    return x


def _bits(count, far_first):
    steps = []
    step = 1
    while step < count:
        steps.append(step)
        step *= 2
    return steps[::-1] if far_first else steps


def _direct_sum(x, axis):
    count = lax.axis_size(axis)
    if count != 4:
        return _butterfly_sum(x, axis)
    got = [lax.ppermute(x, axis, [(i, i ^ k) for i in range(count)]) for k in (1, 2, 3)]
    return (x + got[0]) + (got[1] + got[2])


def _butterfly_gather(x, plan):
    x = x[None]
    for axis, step, slot in plan:
        count = lax.axis_size(axis)
        low = (lax.axis_index(axis) & step) == 0
        other = lax.ppermute(x, axis, [(i, i ^ step) for i in range(count)])
        below = 2 ** sum(1 for _, _, done in plan[: plan.index((axis, step, slot))] if done < slot)
        mine = x.reshape((-1, 1, below) + x.shape[1:])
        theirs = other.reshape(mine.shape)
        first = jnp.where(low, 0, 1)
        both = jnp.zeros((mine.shape[0], 2) + mine.shape[2:], x.dtype)
        both = lax.dynamic_update_slice_in_dim(both, mine, first, 1)
        both = lax.dynamic_update_slice_in_dim(both, theirs, 1 - first, 1)
        x = both.reshape((-1,) + x.shape[1:])
    return x


def _halving_sum(x, axis):
    count = lax.axis_size(axis)
    if count & (count - 1) or x.shape[0] % count:
        return _butterfly_sum(x, axis)
    here = lax.axis_index(axis)
    steps = _bits(count, False)
    for step in steps:
        half = x.shape[0] // 2
        low = (here & step) == 0
        keep = jnp.where(low, x[:half], x[half:])
        give = jnp.where(low, x[half:], x[:half])
        x = keep + lax.ppermute(give, axis, [(i, i ^ step) for i in range(count)])
    for step in steps[::-1]:
        low = (here & step) == 0
        other = lax.ppermute(x, axis, [(i, i ^ step) for i in range(count)])
        first = jnp.where(low, 0, x.shape[0])
        both = jnp.zeros((2 * x.shape[0],) + x.shape[1:], x.dtype)
        both = lax.dynamic_update_slice_in_dim(both, x, first, 0)
        x = lax.dynamic_update_slice_in_dim(both, other, x.shape[0] - first, 0)
    return x


def _pair_split_sum(x, axis):
    count = lax.axis_size(axis)
    if count != 4 or x.shape[0] % 2:
        return _butterfly_sum(x, axis)
    pairs = [(i, i ^ 1) for i in range(count)]
    near_low = (lax.axis_index(axis) & 1) == 0
    x = x + lax.ppermute(x, axis, pairs)
    half = x.shape[0] // 2
    mine = jnp.where(near_low, x[:half], x[half:])
    mine = mine + lax.ppermute(mine, axis, [(i, i ^ 2) for i in range(count)])
    other = lax.ppermute(mine, axis, pairs)
    first = jnp.where(near_low, 0, half)
    both = jnp.zeros(x.shape, x.dtype)
    both = lax.dynamic_update_slice_in_dim(both, mine, first, 0)
    return lax.dynamic_update_slice_in_dim(both, other, half - first, 0)


def _scatter_gather_sum(x, axis):
    count = lax.axis_size(axis)
    if count != 4 or x.shape[0] % count:
        return _halving_sum(x, axis)
    here = lax.axis_index(axis)
    quarter = x.shape[0] // count
    parts = x.reshape((count, quarter) + x.shape[1:])
    got = [parts[here]]
    for k in (1, 2, 3):
        got.append(lax.ppermute(parts[here ^ k], axis, [(i, i ^ k) for i in range(count)]))
    got = jnp.stack(got)
    terms = [got[here ^ j] for j in range(count)]
    mine = (terms[0] + terms[1]) + (terms[2] + terms[3])
    whole = jnp.zeros(parts.shape, x.dtype)
    whole = lax.dynamic_update_slice_in_dim(whole, mine[None], here, 0)
    for k in (1, 2, 3):
        other = lax.ppermute(mine, axis, [(i, i ^ k) for i in range(count)])
        whole = lax.dynamic_update_slice_in_dim(whole, other[None], here ^ k, 0)
    return whole.reshape(x.shape)


def _lower_factor(image, gram_axis):
    gram_part = jnp.dot(
        image.T, image, precision=lax.Precision.HIGHEST, preferred_element_type=jnp.float32
    )
    return jnp.linalg.cholesky(_direct_sum(gram_part, gram_axis))


def _right_solve(lower_factor, image):
    return jax.scipy.linalg.solve_triangular(lower_factor, image.T, lower=True).T


def shards(snapshots, focus_in, focus_out, start_basis):
    rows_here, bins_here, snaps_here = snapshots.shape
    bin_count = lax.axis_size("bin")
    row_count = lax.axis_size("row")
    col_count = lax.axis_size("col")
    col_here = lax.axis_index("col")
    row_here = lax.axis_index("row")
    partial_proj = jnp.einsum(
        "mbs,bmr->brs", snapshots, focus_in, preferred_element_type=jnp.float32
    )
    projected = _direct_sum(partial_proj, "row").astype(jnp.bfloat16)
    lifted = jnp.einsum("bmr,brs->mbs", focus_out, projected, preferred_element_type=jnp.float32)
    focused = (snapshots.astype(jnp.float32) + lifted).astype(jnp.bfloat16)
    columns = bins_here * snaps_here
    local_rows = focused.reshape(rows_here, columns)
    array_size = rows_here * row_count
    col_block = array_size // col_count
    scaling = 1.0 / (columns * col_count * bin_count)

    power_of_two = all(n & (n - 1) == 0 for n in (bin_count, row_count, col_count))
    if row_count == col_count and power_of_two:
        swapped = lax.ppermute(local_rows, ("row", "col"), _transpose_pairs(row_count, col_count))
        swapped = jnp.where(row_here == col_here, local_rows, swapped)
        group = _bits(col_count, True)
        bins = _bits(bin_count, True)
        right_plan = [("col", step, k) for k, step in enumerate(group)]
        right_plan += [("bin", step, len(group) + k) for k, step in enumerate(bins)]
        left_plan = [("bin", step, len(group) + k) for k, step in enumerate(bins)]
        left_plan += [("row", step, k) for k, step in enumerate(group)]
        half = rows_here // 2
        early_bin = [step for step in right_plan if step[0] == "bin"]
        early_bin += [step for step in right_plan if step[0] != "bin"]
        right_rows = jnp.concatenate(
            [
                _butterfly_gather(local_rows[:half], right_plan),
                _butterfly_gather(local_rows[half:], early_bin),
            ],
            1,
        )
        left_rows = _butterfly_gather(swapped, left_plan)
    else:
        right_rows = lax.all_gather(local_rows, ("bin", "col"), axis=0, tiled=False)
        every_row = lax.all_gather(right_rows, "row", axis=1, tiled=True)
        left_rows = lax.dynamic_slice_in_dim(every_row, col_here * col_block, col_block, 1)
    covariance = lax.dot_general(
        left_rows, right_rows, (((0, 2), (0, 2)), ((), ())), preferred_element_type=jnp.float32
    ) * scaling
    covariance_t = lax.dot_general(
        right_rows, left_rows, (((0, 2), (0, 2)), ((), ())), preferred_element_type=jnp.float32
    ) * scaling

    def cov_times(block, on_rows):
        if on_rows:
            partial_image = jnp.dot(
                covariance, block, precision=lax.Precision.HIGHEST,
                preferred_element_type=jnp.float32,
            )
            return _scatter_gather_sum(partial_image, "row")
        partial_image = jnp.dot(
            covariance_t, block, precision=lax.Precision.HIGHEST,
            preferred_element_type=jnp.float32,
        )
        return _scatter_gather_sum(partial_image, "col")

    basis_rows = lax.dynamic_slice_in_dim(start_basis, row_here * rows_here, rows_here, 0)
    image = cov_times(basis_rows, True)
    on_rows = False
    for sweep_index in range(ITERS):
        lower_factor = _lower_factor(image, "row" if on_rows else "col")
        if sweep_index == ITERS - 1:
            basis_rows = _right_solve(lower_factor, image)
            break
        image = _right_solve(lower_factor, cov_times(image, on_rows))
        on_rows = not on_rows
    if not on_rows:
        swapped = lax.ppermute(basis_rows, ("row", "col"), _transpose_pairs(row_count, col_count))
        basis_rows = jnp.where(row_here == col_here, basis_rows, swapped)
    out_rows = array_size // (row_count * col_count)
    basis_out = lax.dynamic_slice_in_dim(basis_rows, col_here * out_rows, out_rows, 0) * math.sqrt(array_size)
    return (covariance, basis_out)


def solution(mesh):
    in_specs = (P("row", "bin", "col"), P("bin", "row", None), P("bin", "row", None), P())
    out_specs = (P("col", "row"), P(("row", "col"), None))
    return jax.shard_map(shards, mesh=mesh, in_specs=in_specs, out_specs=out_specs, check_vma=False)
```

```python
import math

import jax
import jax.numpy as jnp
from jax import lax
from jax.sharding import PartitionSpec as P

ITERS = 2


def _transpose_pairs(row_count, col_count):
    return [
        (i * col_count + j, j * row_count + i)
        for i in range(row_count)
        for j in range(col_count)
        if i != j
    ]


def _butterfly_sum(x, axis):
    count = lax.axis_size(axis)
    if count & (count - 1):
        return lax.psum(x, axis)
    step = 1
    while step < count:
        x = x + lax.ppermute(x, axis, [(i, i ^ step) for i in range(count)])
        step *= 2
    return x


def _bits(count, far_first):
    steps = []
    step = 1
    while step < count:
        steps.append(step)
        step *= 2
    return steps[::-1] if far_first else steps


def _direct_sum(x, axis):
    count = lax.axis_size(axis)
    if count != 4:
        return _butterfly_sum(x, axis)
    got = [lax.ppermute(x, axis, [(i, i ^ k) for i in range(count)]) for k in (1, 2, 3)]
    return (x + got[0]) + (got[1] + got[2])


def _butterfly_gather(x, plan):
    x = x[None]
    for axis, step, slot in plan:
        count = lax.axis_size(axis)
        low = (lax.axis_index(axis) & step) == 0
        other = lax.ppermute(x, axis, [(i, i ^ step) for i in range(count)])
        below = 2 ** sum(1 for _, _, done in plan[: plan.index((axis, step, slot))] if done < slot)
        mine = x.reshape((-1, 1, below) + x.shape[1:])
        theirs = other.reshape(mine.shape)
        first = jnp.where(low, 0, 1)
        both = jnp.zeros((mine.shape[0], 2) + mine.shape[2:], x.dtype)
        both = lax.dynamic_update_slice_in_dim(both, mine, first, 1)
        both = lax.dynamic_update_slice_in_dim(both, theirs, 1 - first, 1)
        x = both.reshape((-1,) + x.shape[1:])
    return x


def _halving_sum(x, axis):
    count = lax.axis_size(axis)
    if count & (count - 1) or x.shape[0] % count:
        return _butterfly_sum(x, axis)
    here = lax.axis_index(axis)
    steps = _bits(count, False)
    for step in steps:
        half = x.shape[0] // 2
        low = (here & step) == 0
        keep = jnp.where(low, x[:half], x[half:])
        give = jnp.where(low, x[half:], x[:half])
        x = keep + lax.ppermute(give, axis, [(i, i ^ step) for i in range(count)])
    for step in steps[::-1]:
        low = (here & step) == 0
        other = lax.ppermute(x, axis, [(i, i ^ step) for i in range(count)])
        first = jnp.where(low, 0, x.shape[0])
        both = jnp.zeros((2 * x.shape[0],) + x.shape[1:], x.dtype)
        both = lax.dynamic_update_slice_in_dim(both, x, first, 0)
        x = lax.dynamic_update_slice_in_dim(both, other, x.shape[0] - first, 0)
    return x


def _pair_split_sum(x, axis):
    count = lax.axis_size(axis)
    if count != 4 or x.shape[0] % 2:
        return _butterfly_sum(x, axis)
    pairs = [(i, i ^ 1) for i in range(count)]
    near_low = (lax.axis_index(axis) & 1) == 0
    x = x + lax.ppermute(x, axis, pairs)
    half = x.shape[0] // 2
    mine = jnp.where(near_low, x[:half], x[half:])
    mine = mine + lax.ppermute(mine, axis, [(i, i ^ 2) for i in range(count)])
    other = lax.ppermute(mine, axis, pairs)
    first = jnp.where(near_low, 0, half)
    both = jnp.zeros(x.shape, x.dtype)
    both = lax.dynamic_update_slice_in_dim(both, mine, first, 0)
    return lax.dynamic_update_slice_in_dim(both, other, half - first, 0)


def _lower_factor(image, gram_axis):
    gram_part = jnp.dot(
        image.T, image, precision=lax.Precision.HIGHEST, preferred_element_type=jnp.float32
    )
    return jnp.linalg.cholesky(_direct_sum(gram_part, gram_axis))


def _right_solve(lower_factor, image):
    return jax.scipy.linalg.solve_triangular(lower_factor, image.T, lower=True).T


def shards(snapshots, focus_in, focus_out, start_basis):
    rows_here, bins_here, snaps_here = snapshots.shape
    bin_count = lax.axis_size("bin")
    row_count = lax.axis_size("row")
    col_count = lax.axis_size("col")
    col_here = lax.axis_index("col")
    row_here = lax.axis_index("row")
    partial_proj = jnp.einsum(
        "mbs,bmr->brs", snapshots, focus_in, preferred_element_type=jnp.float32
    )
    projected = _direct_sum(partial_proj, "row").astype(jnp.bfloat16)
    lifted = jnp.einsum("bmr,brs->mbs", focus_out, projected, preferred_element_type=jnp.float32)
    focused = (snapshots.astype(jnp.float32) + lifted).astype(jnp.bfloat16)
    columns = bins_here * snaps_here
    local_rows = focused.reshape(rows_here, columns)
    array_size = rows_here * row_count
    col_block = array_size // col_count
    scaling = 1.0 / (columns * col_count * bin_count)

    power_of_two = all(n & (n - 1) == 0 for n in (bin_count, row_count, col_count))
    if row_count == col_count and power_of_two:
        swapped = lax.ppermute(local_rows, ("row", "col"), _transpose_pairs(row_count, col_count))
        swapped = jnp.where(row_here == col_here, local_rows, swapped)
        group = _bits(col_count, True)
        bins = _bits(bin_count, True)
        right_plan = [("col", step, k) for k, step in enumerate(group)]
        right_plan += [("bin", step, len(group) + k) for k, step in enumerate(bins)]
        left_plan = [("bin", step, len(group) + k) for k, step in enumerate(bins)]
        left_plan += [("row", step, k) for k, step in enumerate(group)]
        half = rows_here // 2
        early_bin = [step for step in right_plan if step[0] == "bin"]
        early_bin += [step for step in right_plan if step[0] != "bin"]
        right_rows = jnp.concatenate(
            [
                _butterfly_gather(local_rows[:half], right_plan),
                _butterfly_gather(local_rows[half:], early_bin),
            ],
            1,
        )
        left_rows = jnp.concatenate(
            [
                _butterfly_gather(swapped[:half], left_plan),
                _butterfly_gather(swapped[half:], left_plan),
            ],
            1,
        )
    else:
        right_rows = lax.all_gather(local_rows, ("bin", "col"), axis=0, tiled=False)
        every_row = lax.all_gather(right_rows, "row", axis=1, tiled=True)
        left_rows = lax.dynamic_slice_in_dim(every_row, col_here * col_block, col_block, 1)
    covariance = lax.dot_general(
        left_rows, right_rows, (((0, 2), (0, 2)), ((), ())), preferred_element_type=jnp.float32
    ) * scaling
    covariance_t = lax.dot_general(
        right_rows, left_rows, (((0, 2), (0, 2)), ((), ())), preferred_element_type=jnp.float32
    ) * scaling

    def cov_times(block, on_rows):
        if on_rows:
            partial_image = jnp.dot(
                covariance, block, precision=lax.Precision.HIGHEST,
                preferred_element_type=jnp.float32,
            )
            return _pair_split_sum(partial_image, "row")
        partial_image = jnp.dot(
            covariance_t, block, precision=lax.Precision.HIGHEST,
            preferred_element_type=jnp.float32,
        )
        return _halving_sum(partial_image, "col")

    basis_rows = lax.dynamic_slice_in_dim(start_basis, row_here * rows_here, rows_here, 0)
    image = cov_times(basis_rows, True)
    on_rows = False
    for sweep_index in range(ITERS):
        lower_factor = _lower_factor(image, "row" if on_rows else "col")
        if sweep_index == ITERS - 1:
            basis_rows = _right_solve(lower_factor, image)
            break
        image = _right_solve(lower_factor, cov_times(image, on_rows))
        on_rows = not on_rows
    if not on_rows:
        swapped = lax.ppermute(basis_rows, ("row", "col"), _transpose_pairs(row_count, col_count))
        basis_rows = jnp.where(row_here == col_here, basis_rows, swapped)
    out_rows = array_size // (row_count * col_count)
    basis_out = lax.dynamic_slice_in_dim(basis_rows, col_here * out_rows, out_rows, 0) * math.sqrt(array_size)
    return (covariance, basis_out)


def solution(mesh):
    in_specs = (P("row", "bin", "col"), P("bin", "row", None), P("bin", "row", None), P())
    out_specs = (P("col", "row"), P(("row", "col"), None))
    return jax.shard_map(shards, mesh=mesh, in_specs=in_specs, out_specs=out_specs, check_vma=False)
```

```python
import math

import jax
import jax.numpy as jnp
from jax import lax
from jax.sharding import PartitionSpec as P

ITERS = 2


def _transpose_pairs(row_count, col_count):
    return [
        (i * col_count + j, j * row_count + i)
        for i in range(row_count)
        for j in range(col_count)
        if i != j
    ]


def _butterfly_sum(x, axis):
    count = lax.axis_size(axis)
    if count & (count - 1):
        return lax.psum(x, axis)
    step = 1
    while step < count:
        x = x + lax.ppermute(x, axis, [(i, i ^ step) for i in range(count)])
        step *= 2
    return x


def _bits(count, far_first):
    steps = []
    step = 1
    while step < count:
        steps.append(step)
        step *= 2
    return steps[::-1] if far_first else steps


def _direct_sum(x, axis):
    count = lax.axis_size(axis)
    if count != 4:
        return _butterfly_sum(x, axis)
    got = [lax.ppermute(x, axis, [(i, i ^ k) for i in range(count)]) for k in (1, 2, 3)]
    return (x + got[0]) + (got[1] + got[2])


def _butterfly_gather(x, plan):
    x = x[None]
    for axis, step, slot in plan:
        count = lax.axis_size(axis)
        low = (lax.axis_index(axis) & step) == 0
        other = lax.ppermute(x, axis, [(i, i ^ step) for i in range(count)])
        below = 2 ** sum(1 for _, _, done in plan[: plan.index((axis, step, slot))] if done < slot)
        mine = x.reshape((-1, 1, below) + x.shape[1:])
        theirs = other.reshape(mine.shape)
        first = jnp.where(low, 0, 1)
        both = jnp.zeros((mine.shape[0], 2) + mine.shape[2:], x.dtype)
        both = lax.dynamic_update_slice_in_dim(both, mine, first, 1)
        both = lax.dynamic_update_slice_in_dim(both, theirs, 1 - first, 1)
        x = both.reshape((-1,) + x.shape[1:])
    return x


def _halving_sum(x, axis):
    count = lax.axis_size(axis)
    if count & (count - 1) or x.shape[0] % count:
        return _butterfly_sum(x, axis)
    here = lax.axis_index(axis)
    steps = _bits(count, False)
    for step in steps:
        half = x.shape[0] // 2
        low = (here & step) == 0
        keep = jnp.where(low, x[:half], x[half:])
        give = jnp.where(low, x[half:], x[:half])
        x = keep + lax.ppermute(give, axis, [(i, i ^ step) for i in range(count)])
    for step in steps[::-1]:
        low = (here & step) == 0
        other = lax.ppermute(x, axis, [(i, i ^ step) for i in range(count)])
        first = jnp.where(low, 0, x.shape[0])
        both = jnp.zeros((2 * x.shape[0],) + x.shape[1:], x.dtype)
        both = lax.dynamic_update_slice_in_dim(both, x, first, 0)
        x = lax.dynamic_update_slice_in_dim(both, other, x.shape[0] - first, 0)
    return x


def _pair_split_sum(x, axis):
    count = lax.axis_size(axis)
    if count != 4 or x.shape[0] % 2:
        return _butterfly_sum(x, axis)
    pairs = [(i, i ^ 1) for i in range(count)]
    near_low = (lax.axis_index(axis) & 1) == 0
    x = x + lax.ppermute(x, axis, pairs)
    half = x.shape[0] // 2
    mine = jnp.where(near_low, x[:half], x[half:])
    mine = mine + lax.ppermute(mine, axis, [(i, i ^ 2) for i in range(count)])
    other = lax.ppermute(mine, axis, pairs)
    first = jnp.where(near_low, 0, half)
    both = jnp.zeros(x.shape, x.dtype)
    both = lax.dynamic_update_slice_in_dim(both, mine, first, 0)
    return lax.dynamic_update_slice_in_dim(both, other, half - first, 0)


def _lower_factor(image, gram_axis):
    gram_part = jnp.dot(
        image.T, image, precision=lax.Precision.HIGHEST, preferred_element_type=jnp.float32
    )
    return jnp.linalg.cholesky(_direct_sum(gram_part, gram_axis))


def _right_solve(lower_factor, image):
    return lax.linalg.triangular_solve(
        lower_factor, image, left_side=False, lower=True, transpose_a=True
    )


def shards(snapshots, focus_in, focus_out, start_basis):
    rows_here, bins_here, snaps_here = snapshots.shape
    bin_count = lax.axis_size("bin")
    row_count = lax.axis_size("row")
    col_count = lax.axis_size("col")
    col_here = lax.axis_index("col")
    row_here = lax.axis_index("row")
    partial_proj = jnp.einsum(
        "mbs,bmr->brs", snapshots, focus_in, preferred_element_type=jnp.float32
    )
    projected = _direct_sum(partial_proj, "row").astype(jnp.bfloat16)
    lifted = jnp.einsum("bmr,brs->mbs", focus_out, projected, preferred_element_type=jnp.float32)
    focused = (snapshots.astype(jnp.float32) + lifted).astype(jnp.bfloat16)
    columns = bins_here * snaps_here
    local_rows = focused.reshape(rows_here, columns)
    array_size = rows_here * row_count
    col_block = array_size // col_count
    scaling = 1.0 / (columns * col_count * bin_count)

    power_of_two = all(n & (n - 1) == 0 for n in (bin_count, row_count, col_count))
    if row_count == col_count and power_of_two:
        swapped = lax.ppermute(local_rows, ("row", "col"), _transpose_pairs(row_count, col_count))
        swapped = jnp.where(row_here == col_here, local_rows, swapped)
        group = _bits(col_count, True)
        bins = _bits(bin_count, True)
        right_plan = [("col", step, k) for k, step in enumerate(group)]
        right_plan += [("bin", step, len(group) + k) for k, step in enumerate(bins)]
        left_plan = [("bin", step, len(group) + k) for k, step in enumerate(bins)]
        left_plan += [("row", step, k) for k, step in enumerate(group)]
        half = rows_here // 2
        early_bin = [step for step in right_plan if step[0] == "bin"]
        early_bin += [step for step in right_plan if step[0] != "bin"]
        right_rows = jnp.concatenate(
            [
                _butterfly_gather(local_rows[:half], right_plan),
                _butterfly_gather(local_rows[half:], early_bin),
            ],
            1,
        )
        left_rows = jnp.concatenate(
            [
                _butterfly_gather(swapped[:half], left_plan),
                _butterfly_gather(swapped[half:], left_plan),
            ],
            1,
        )
    else:
        right_rows = lax.all_gather(local_rows, ("bin", "col"), axis=0, tiled=False)
        every_row = lax.all_gather(right_rows, "row", axis=1, tiled=True)
        left_rows = lax.dynamic_slice_in_dim(every_row, col_here * col_block, col_block, 1)
    covariance = lax.dot_general(
        left_rows, right_rows, (((0, 2), (0, 2)), ((), ())), preferred_element_type=jnp.float32
    ) * scaling
    covariance_t = lax.dot_general(
        right_rows, left_rows, (((0, 2), (0, 2)), ((), ())), preferred_element_type=jnp.float32
    ) * scaling

    def cov_times(block, on_rows):
        if on_rows:
            partial_image = jnp.dot(
                covariance, block, precision=lax.Precision.HIGHEST,
                preferred_element_type=jnp.float32,
            )
            return _pair_split_sum(partial_image, "row")
        partial_image = jnp.dot(
            covariance_t, block, precision=lax.Precision.HIGHEST,
            preferred_element_type=jnp.float32,
        )
        return _halving_sum(partial_image, "col")

    basis_rows = lax.dynamic_slice_in_dim(start_basis, row_here * rows_here, rows_here, 0)
    image = cov_times(basis_rows, True)
    on_rows = False
    for sweep_index in range(ITERS):
        lower_factor = _lower_factor(image, "row" if on_rows else "col")
        if sweep_index == ITERS - 1:
            basis_rows = _right_solve(lower_factor, image)
            break
        image = _right_solve(lower_factor, cov_times(image, on_rows))
        on_rows = not on_rows
    if not on_rows:
        swapped = lax.ppermute(basis_rows, ("row", "col"), _transpose_pairs(row_count, col_count))
        basis_rows = jnp.where(row_here == col_here, basis_rows, swapped)
    out_rows = array_size // (row_count * col_count)
    basis_out = lax.dynamic_slice_in_dim(basis_rows, col_here * out_rows, out_rows, 0) * math.sqrt(array_size)
    return (covariance, basis_out)


def solution(mesh):
    in_specs = (P("row", "bin", "col"), P("bin", "row", None), P("bin", "row", None), P())
    out_specs = (P("col", "row"), P(("row", "col"), None))
    return jax.shard_map(shards, mesh=mesh, in_specs=in_specs, out_specs=out_specs, check_vma=False)
```

```python
import math

import jax
import jax.numpy as jnp
from jax import lax
from jax.sharding import PartitionSpec as P

ITERS = 2


def _transpose_pairs(row_count, col_count):
    return [
        (i * col_count + j, j * row_count + i)
        for i in range(row_count)
        for j in range(col_count)
        if i != j
    ]


def _butterfly_sum(x, axis):
    count = lax.axis_size(axis)
    if count & (count - 1):
        return lax.psum(x, axis)
    step = 1
    while step < count:
        x = x + lax.ppermute(x, axis, [(i, i ^ step) for i in range(count)])
        step *= 2
    return x


def _bits(count, far_first):
    steps = []
    step = 1
    while step < count:
        steps.append(step)
        step *= 2
    return steps[::-1] if far_first else steps


def _direct_sum(x, axis):
    count = lax.axis_size(axis)
    if count != 4:
        return _butterfly_sum(x, axis)
    got = [lax.ppermute(x, axis, [(i, i ^ k) for i in range(count)]) for k in (1, 2, 3)]
    return (x + got[0]) + (got[1] + got[2])


def _butterfly_gather(x, plan):
    x = x[None]
    for axis, step, slot in plan:
        count = lax.axis_size(axis)
        low = (lax.axis_index(axis) & step) == 0
        other = lax.ppermute(x, axis, [(i, i ^ step) for i in range(count)])
        below = 2 ** sum(1 for _, _, done in plan[: plan.index((axis, step, slot))] if done < slot)
        mine = x.reshape((-1, 1, below) + x.shape[1:])
        theirs = other.reshape(mine.shape)
        first = jnp.where(low, 0, 1)
        both = jnp.zeros((mine.shape[0], 2) + mine.shape[2:], x.dtype)
        both = lax.dynamic_update_slice_in_dim(both, mine, first, 1)
        both = lax.dynamic_update_slice_in_dim(both, theirs, 1 - first, 1)
        x = both.reshape((-1,) + x.shape[1:])
    return x


def _halving_sum(x, axis):
    count = lax.axis_size(axis)
    if count & (count - 1) or x.shape[0] % count:
        return _butterfly_sum(x, axis)
    here = lax.axis_index(axis)
    steps = _bits(count, False)
    for step in steps:
        half = x.shape[0] // 2
        low = (here & step) == 0
        keep = jnp.where(low, x[:half], x[half:])
        give = jnp.where(low, x[half:], x[:half])
        x = keep + lax.ppermute(give, axis, [(i, i ^ step) for i in range(count)])
    for step in steps[::-1]:
        low = (here & step) == 0
        other = lax.ppermute(x, axis, [(i, i ^ step) for i in range(count)])
        first = jnp.where(low, 0, x.shape[0])
        both = jnp.zeros((2 * x.shape[0],) + x.shape[1:], x.dtype)
        both = lax.dynamic_update_slice_in_dim(both, x, first, 0)
        x = lax.dynamic_update_slice_in_dim(both, other, x.shape[0] - first, 0)
    return x


def _pair_split_sum(x, axis):
    count = lax.axis_size(axis)
    if count != 4 or x.shape[0] % 2:
        return _butterfly_sum(x, axis)
    pairs = [(i, i ^ 1) for i in range(count)]
    near_low = (lax.axis_index(axis) & 1) == 0
    x = x + lax.ppermute(x, axis, pairs)
    half = x.shape[0] // 2
    mine = jnp.where(near_low, x[:half], x[half:])
    mine = mine + lax.ppermute(mine, axis, [(i, i ^ 2) for i in range(count)])
    other = lax.ppermute(mine, axis, pairs)
    first = jnp.where(near_low, 0, half)
    both = jnp.zeros(x.shape, x.dtype)
    both = lax.dynamic_update_slice_in_dim(both, mine, first, 0)
    return lax.dynamic_update_slice_in_dim(both, other, half - first, 0)


def _lower_factor(image, gram_axis):
    gram_part = jnp.dot(
        image.T, image, precision=lax.Precision.HIGHEST, preferred_element_type=jnp.float32
    )
    return jnp.linalg.cholesky(_direct_sum(gram_part, gram_axis))


def _right_solve(lower_factor, image):
    return jax.scipy.linalg.solve_triangular(lower_factor, image.T, lower=True).T


def shards(snapshots, focus_in, focus_out, start_basis):
    rows_here, bins_here, snaps_here = snapshots.shape
    bin_count = lax.axis_size("bin")
    row_count = lax.axis_size("row")
    col_count = lax.axis_size("col")
    col_here = lax.axis_index("col")
    row_here = lax.axis_index("row")
    partial_proj = jnp.einsum(
        "mbs,bmr->brs", snapshots, focus_in, preferred_element_type=jnp.float32
    )
    projected = _direct_sum(partial_proj, "row").astype(jnp.bfloat16)
    lifted = jnp.einsum("bmr,brs->mbs", focus_out, projected, preferred_element_type=jnp.float32)
    focused = (snapshots.astype(jnp.float32) + lifted).astype(jnp.bfloat16)
    columns = bins_here * snaps_here
    local_rows = focused.reshape(rows_here, columns)
    array_size = rows_here * row_count
    col_block = array_size // col_count
    scaling = 1.0 / (columns * col_count * bin_count)

    power_of_two = all(n & (n - 1) == 0 for n in (bin_count, row_count, col_count))
    if row_count == col_count and power_of_two:
        swapped = lax.ppermute(local_rows, ("row", "col"), _transpose_pairs(row_count, col_count))
        swapped = jnp.where(row_here == col_here, local_rows, swapped)
        group = _bits(col_count, True)
        bins = _bits(bin_count, True)
        right_plan = [("col", step, k) for k, step in enumerate(group)]
        right_plan += [("bin", step, len(group) + k) for k, step in enumerate(bins)]
        left_plan = [("bin", step, len(group) + k) for k, step in enumerate(bins)]
        left_plan += [("row", step, k) for k, step in enumerate(group)]
        half = rows_here // 2
        early_bin = [step for step in right_plan if step[0] == "bin"]
        early_bin += [step for step in right_plan if step[0] != "bin"]
        right_rows = jnp.concatenate(
            [
                _butterfly_gather(local_rows[:half], right_plan),
                _butterfly_gather(local_rows[half:], early_bin),
            ],
            1,
        )
        x_first = left_plan[len(bins):len(bins) + 1] + left_plan[: len(bins)] + left_plan[len(bins) + 1:]
        left_rows = jnp.concatenate(
            [
                _butterfly_gather(swapped[:half], left_plan),
                _butterfly_gather(swapped[half:], x_first),
            ],
            1,
        )
    else:
        right_rows = lax.all_gather(local_rows, ("bin", "col"), axis=0, tiled=False)
        every_row = lax.all_gather(right_rows, "row", axis=1, tiled=True)
        left_rows = lax.dynamic_slice_in_dim(every_row, col_here * col_block, col_block, 1)
    covariance = lax.dot_general(
        left_rows, right_rows, (((0, 2), (0, 2)), ((), ())), preferred_element_type=jnp.float32
    ) * scaling
    covariance_t = lax.dot_general(
        right_rows, left_rows, (((0, 2), (0, 2)), ((), ())), preferred_element_type=jnp.float32
    ) * scaling

    def cov_times(block, on_rows):
        if on_rows:
            partial_image = jnp.dot(
                covariance, block, precision=lax.Precision.HIGHEST,
                preferred_element_type=jnp.float32,
            )
            return _pair_split_sum(partial_image, "row")
        partial_image = jnp.dot(
            covariance_t, block, precision=lax.Precision.HIGHEST,
            preferred_element_type=jnp.float32,
        )
        return _halving_sum(partial_image, "col")

    basis_rows = lax.dynamic_slice_in_dim(start_basis, row_here * rows_here, rows_here, 0)
    image = cov_times(basis_rows, True)
    on_rows = False
    for sweep_index in range(ITERS):
        lower_factor = _lower_factor(image, "row" if on_rows else "col")
        if sweep_index == ITERS - 1:
            basis_rows = _right_solve(lower_factor, image)
            break
        image = _right_solve(lower_factor, cov_times(image, on_rows))
        on_rows = not on_rows
    if not on_rows:
        swapped = lax.ppermute(basis_rows, ("row", "col"), _transpose_pairs(row_count, col_count))
        basis_rows = jnp.where(row_here == col_here, basis_rows, swapped)
    out_rows = array_size // (row_count * col_count)
    basis_out = lax.dynamic_slice_in_dim(basis_rows, col_here * out_rows, out_rows, 0) * math.sqrt(array_size)
    return (covariance, basis_out)


def solution(mesh):
    in_specs = (P("row", "bin", "col"), P("bin", "row", None), P("bin", "row", None), P())
    out_specs = (P("col", "row"), P(("row", "col"), None))
    return jax.shard_map(shards, mesh=mesh, in_specs=in_specs, out_specs=out_specs, check_vma=False)
```

```python
import math

import jax
import jax.numpy as jnp
from jax import lax
from jax.sharding import PartitionSpec as P

ITERS = 2


def _transpose_pairs(row_count, col_count):
    return [
        (i * col_count + j, j * row_count + i)
        for i in range(row_count)
        for j in range(col_count)
        if i != j
    ]


def _butterfly_sum(x, axis):
    count = lax.axis_size(axis)
    if count & (count - 1):
        return lax.psum(x, axis)
    step = 1
    while step < count:
        x = x + lax.ppermute(x, axis, [(i, i ^ step) for i in range(count)])
        step *= 2
    return x


def _bits(count, far_first):
    steps = []
    step = 1
    while step < count:
        steps.append(step)
        step *= 2
    return steps[::-1] if far_first else steps


def _direct_sum(x, axis):
    count = lax.axis_size(axis)
    if count != 4:
        return _butterfly_sum(x, axis)
    got = [lax.ppermute(x, axis, [(i, i ^ k) for i in range(count)]) for k in (1, 2, 3)]
    return (x + got[0]) + (got[1] + got[2])


def _butterfly_gather(x, plan):
    x = x[None]
    for axis, step, slot in plan:
        count = lax.axis_size(axis)
        low = (lax.axis_index(axis) & step) == 0
        other = lax.ppermute(x, axis, [(i, i ^ step) for i in range(count)])
        below = 2 ** sum(1 for _, _, done in plan[: plan.index((axis, step, slot))] if done < slot)
        mine = x.reshape((-1, 1, below) + x.shape[1:])
        theirs = other.reshape(mine.shape)
        first = jnp.where(low, 0, 1)
        both = jnp.zeros((mine.shape[0], 2) + mine.shape[2:], x.dtype)
        both = lax.dynamic_update_slice_in_dim(both, mine, first, 1)
        both = lax.dynamic_update_slice_in_dim(both, theirs, 1 - first, 1)
        x = both.reshape((-1,) + x.shape[1:])
    return x


def _halving_sum(x, axis):
    count = lax.axis_size(axis)
    if count & (count - 1) or x.shape[0] % count:
        return _butterfly_sum(x, axis)
    here = lax.axis_index(axis)
    steps = _bits(count, False)
    for step in steps:
        half = x.shape[0] // 2
        low = (here & step) == 0
        keep = jnp.where(low, x[:half], x[half:])
        give = jnp.where(low, x[half:], x[:half])
        x = keep + lax.ppermute(give, axis, [(i, i ^ step) for i in range(count)])
    for step in steps[::-1]:
        low = (here & step) == 0
        other = lax.ppermute(x, axis, [(i, i ^ step) for i in range(count)])
        first = jnp.where(low, 0, x.shape[0])
        both = jnp.zeros((2 * x.shape[0],) + x.shape[1:], x.dtype)
        both = lax.dynamic_update_slice_in_dim(both, x, first, 0)
        x = lax.dynamic_update_slice_in_dim(both, other, x.shape[0] - first, 0)
    return x


def _pair_split_sum(x, axis):
    count = lax.axis_size(axis)
    if count != 4 or x.shape[0] % 2:
        return _butterfly_sum(x, axis)
    pairs = [(i, i ^ 1) for i in range(count)]
    near_low = (lax.axis_index(axis) & 1) == 0
    x = x + lax.ppermute(x, axis, pairs)
    half = x.shape[0] // 2
    mine = jnp.where(near_low, x[:half], x[half:])
    mine = mine + lax.ppermute(mine, axis, [(i, i ^ 2) for i in range(count)])
    other = lax.ppermute(mine, axis, pairs)
    first = jnp.where(near_low, 0, half)
    both = jnp.zeros(x.shape, x.dtype)
    both = lax.dynamic_update_slice_in_dim(both, mine, first, 0)
    return lax.dynamic_update_slice_in_dim(both, other, half - first, 0)


def _lower_factor(image, gram_axis):
    gram_part = jnp.dot(
        image.T, image, precision=lax.Precision.HIGHEST, preferred_element_type=jnp.float32
    )
    return jnp.linalg.cholesky(_direct_sum(gram_part, gram_axis))


def _right_solve(lower_factor, image):
    return jax.scipy.linalg.solve_triangular(lower_factor, image.T, lower=True).T


def shards(snapshots, focus_in, focus_out, start_basis):
    rows_here, bins_here, snaps_here = snapshots.shape
    bin_count = lax.axis_size("bin")
    row_count = lax.axis_size("row")
    col_count = lax.axis_size("col")
    col_here = lax.axis_index("col")
    row_here = lax.axis_index("row")
    partial_proj = jnp.einsum(
        "mbs,bmr->brs", snapshots, focus_in, preferred_element_type=jnp.float32
    )
    projected = _direct_sum(partial_proj, "row").astype(jnp.bfloat16)
    lifted = jnp.einsum("bmr,brs->mbs", focus_out, projected, preferred_element_type=jnp.float32)
    focused = (snapshots.astype(jnp.float32) + lifted).astype(jnp.bfloat16)
    columns = bins_here * snaps_here
    local_rows = focused.reshape(rows_here, columns)
    array_size = rows_here * row_count
    col_block = array_size // col_count
    scaling = 1.0 / (columns * col_count * bin_count)

    power_of_two = all(n & (n - 1) == 0 for n in (bin_count, row_count, col_count))
    if row_count == col_count and power_of_two:
        swapped = lax.ppermute(local_rows, ("row", "col"), _transpose_pairs(row_count, col_count))
        swapped = jnp.where(row_here == col_here, local_rows, swapped)
        group = _bits(col_count, True)
        bins = _bits(bin_count, True)
        right_plan = [("col", step, k) for k, step in enumerate(group)]
        right_plan += [("bin", step, len(group) + k) for k, step in enumerate(bins)]
        left_plan = [("bin", step, len(group) + k) for k, step in enumerate(bins)]
        left_plan += [("row", step, k) for k, step in enumerate(group)]
        half = rows_here // 2
        early_bin = [step for step in right_plan if step[0] == "bin"]
        early_bin += [step for step in right_plan if step[0] != "bin"]
        z_share = 3 * rows_here // 4 if rows_here % 64 == 0 else half
        right_rows = jnp.concatenate(
            [
                _butterfly_gather(local_rows[:z_share], right_plan),
                _butterfly_gather(local_rows[z_share:], early_bin),
            ],
            1,
        )
        left_rows = jnp.concatenate(
            [
                _butterfly_gather(swapped[:half], left_plan),
                _butterfly_gather(swapped[half:], left_plan),
            ],
            1,
        )
    else:
        right_rows = lax.all_gather(local_rows, ("bin", "col"), axis=0, tiled=False)
        every_row = lax.all_gather(right_rows, "row", axis=1, tiled=True)
        left_rows = lax.dynamic_slice_in_dim(every_row, col_here * col_block, col_block, 1)
    covariance = lax.dot_general(
        left_rows, right_rows, (((0, 2), (0, 2)), ((), ())), preferred_element_type=jnp.float32
    ) * scaling
    covariance_t = lax.dot_general(
        right_rows, left_rows, (((0, 2), (0, 2)), ((), ())), preferred_element_type=jnp.float32
    ) * scaling

    def cov_times(block, on_rows):
        if on_rows:
            partial_image = jnp.dot(
                covariance, block, precision=lax.Precision.HIGHEST,
                preferred_element_type=jnp.float32,
            )
            return _pair_split_sum(partial_image, "row")
        partial_image = jnp.dot(
            covariance_t, block, precision=lax.Precision.HIGHEST,
            preferred_element_type=jnp.float32,
        )
        return _halving_sum(partial_image, "col")

    basis_rows = lax.dynamic_slice_in_dim(start_basis, row_here * rows_here, rows_here, 0)
    image = cov_times(basis_rows, True)
    on_rows = False
    for sweep_index in range(ITERS):
        lower_factor = _lower_factor(image, "row" if on_rows else "col")
        if sweep_index == ITERS - 1:
            basis_rows = _right_solve(lower_factor, image)
            break
        image = _right_solve(lower_factor, cov_times(image, on_rows))
        on_rows = not on_rows
    if not on_rows:
        swapped = lax.ppermute(basis_rows, ("row", "col"), _transpose_pairs(row_count, col_count))
        basis_rows = jnp.where(row_here == col_here, basis_rows, swapped)
    out_rows = array_size // (row_count * col_count)
    basis_out = lax.dynamic_slice_in_dim(basis_rows, col_here * out_rows, out_rows, 0) * math.sqrt(array_size)
    return (covariance, basis_out)


def solution(mesh):
    in_specs = (P("row", "bin", "col"), P("bin", "row", None), P("bin", "row", None), P())
    out_specs = (P("col", "row"), P(("row", "col"), None))
    return jax.shard_map(shards, mesh=mesh, in_specs=in_specs, out_specs=out_specs, check_vma=False)
```

```python
import math

import jax
import jax.numpy as jnp
from jax import lax
from jax.sharding import PartitionSpec as P

ITERS = 2


def _transpose_pairs(row_count, col_count):
    return [
        (i * col_count + j, j * row_count + i)
        for i in range(row_count)
        for j in range(col_count)
        if i != j
    ]


def _butterfly_sum(x, axis):
    count = lax.axis_size(axis)
    if count & (count - 1):
        return lax.psum(x, axis)
    step = 1
    while step < count:
        x = x + lax.ppermute(x, axis, [(i, i ^ step) for i in range(count)])
        step *= 2
    return x


def _bits(count, far_first):
    steps = []
    step = 1
    while step < count:
        steps.append(step)
        step *= 2
    return steps[::-1] if far_first else steps


def _direct_sum(x, axis):
    count = lax.axis_size(axis)
    if count != 4:
        return _butterfly_sum(x, axis)
    got = [lax.ppermute(x, axis, [(i, i ^ k) for i in range(count)]) for k in (1, 2, 3)]
    return (x + got[0]) + (got[1] + got[2])


def _butterfly_gather(x, plan):
    x = x[None]
    for axis, step, slot in plan:
        count = lax.axis_size(axis)
        low = (lax.axis_index(axis) & step) == 0
        other = lax.ppermute(x, axis, [(i, i ^ step) for i in range(count)])
        below = 2 ** sum(1 for _, _, done in plan[: plan.index((axis, step, slot))] if done < slot)
        mine = x.reshape((-1, 1, below) + x.shape[1:])
        theirs = other.reshape(mine.shape)
        first = jnp.where(low, 0, 1)
        both = jnp.zeros((mine.shape[0], 2) + mine.shape[2:], x.dtype)
        both = lax.dynamic_update_slice_in_dim(both, mine, first, 1)
        both = lax.dynamic_update_slice_in_dim(both, theirs, 1 - first, 1)
        x = both.reshape((-1,) + x.shape[1:])
    return x


def _halving_sum(x, axis):
    count = lax.axis_size(axis)
    if count & (count - 1) or x.shape[0] % count:
        return _butterfly_sum(x, axis)
    here = lax.axis_index(axis)
    steps = _bits(count, False)
    for step in steps:
        half = x.shape[0] // 2
        low = (here & step) == 0
        keep = jnp.where(low, x[:half], x[half:])
        give = jnp.where(low, x[half:], x[:half])
        x = keep + lax.ppermute(give, axis, [(i, i ^ step) for i in range(count)])
    for step in steps[::-1]:
        low = (here & step) == 0
        other = lax.ppermute(x, axis, [(i, i ^ step) for i in range(count)])
        first = jnp.where(low, 0, x.shape[0])
        both = jnp.zeros((2 * x.shape[0],) + x.shape[1:], x.dtype)
        both = lax.dynamic_update_slice_in_dim(both, x, first, 0)
        x = lax.dynamic_update_slice_in_dim(both, other, x.shape[0] - first, 0)
    return x


def _pair_split_sum(x, axis):
    count = lax.axis_size(axis)
    if count != 4 or x.shape[0] % 2:
        return _butterfly_sum(x, axis)
    pairs = [(i, i ^ 1) for i in range(count)]
    near_low = (lax.axis_index(axis) & 1) == 0
    x = x + lax.ppermute(x, axis, pairs)
    half = x.shape[0] // 2
    mine = jnp.where(near_low, x[:half], x[half:])
    mine = mine + lax.ppermute(mine, axis, [(i, i ^ 2) for i in range(count)])
    other = lax.ppermute(mine, axis, pairs)
    first = jnp.where(near_low, 0, half)
    both = jnp.zeros(x.shape, x.dtype)
    both = lax.dynamic_update_slice_in_dim(both, mine, first, 0)
    return lax.dynamic_update_slice_in_dim(both, other, half - first, 0)


def _lower_factor(image, gram_axis):
    gram_part = jnp.dot(
        image.T, image, precision=lax.Precision.HIGHEST, preferred_element_type=jnp.float32
    )
    return jnp.linalg.cholesky(_direct_sum(gram_part, gram_axis))


def _right_solve(lower_factor, image):
    return jax.scipy.linalg.solve_triangular(lower_factor, image.T, lower=True).T


def shards(snapshots, focus_in, focus_out, start_basis):
    rows_here, bins_here, snaps_here = snapshots.shape
    bin_count = lax.axis_size("bin")
    row_count = lax.axis_size("row")
    col_count = lax.axis_size("col")
    col_here = lax.axis_index("col")
    row_here = lax.axis_index("row")
    partial_proj = jnp.einsum(
        "mbs,bmr->brs", snapshots, focus_in, preferred_element_type=jnp.float32
    )
    projected = _direct_sum(partial_proj, "row").astype(jnp.bfloat16)
    lifted = jnp.einsum("bmr,brs->mbs", focus_out, projected, preferred_element_type=jnp.float32)
    focused = (snapshots.astype(jnp.float32) + lifted).astype(jnp.bfloat16)
    columns = bins_here * snaps_here
    local_rows = focused.reshape(rows_here, columns)
    array_size = rows_here * row_count
    col_block = array_size // col_count
    scaling = 1.0 / (columns * col_count * bin_count)

    power_of_two = all(n & (n - 1) == 0 for n in (bin_count, row_count, col_count))
    if row_count == col_count and power_of_two:
        swapped = lax.ppermute(local_rows, ("row", "col"), _transpose_pairs(row_count, col_count))
        swapped = jnp.where(row_here == col_here, local_rows, swapped)
        group = _bits(col_count, True)
        bins = _bits(bin_count, True)
        right_plan = [("col", step, k) for k, step in enumerate(group)]
        right_plan += [("bin", step, len(group) + k) for k, step in enumerate(bins)]
        left_plan = [("bin", step, len(group) + k) for k, step in enumerate(bins)]
        left_plan += [("row", step, k) for k, step in enumerate(group)]
        half = rows_here // 2
        early_bin = [step for step in right_plan if step[0] == "bin"]
        early_bin += [step for step in right_plan if step[0] != "bin"]
        z_share = 3 * rows_here // 8 if rows_here % 128 == 0 else half
        right_rows = jnp.concatenate(
            [
                _butterfly_gather(local_rows[:z_share], right_plan),
                _butterfly_gather(local_rows[z_share:], early_bin),
            ],
            1,
        )
        left_rows = jnp.concatenate(
            [
                _butterfly_gather(swapped[:half], left_plan),
                _butterfly_gather(swapped[half:], left_plan),
            ],
            1,
        )
    else:
        right_rows = lax.all_gather(local_rows, ("bin", "col"), axis=0, tiled=False)
        every_row = lax.all_gather(right_rows, "row", axis=1, tiled=True)
        left_rows = lax.dynamic_slice_in_dim(every_row, col_here * col_block, col_block, 1)
    covariance = lax.dot_general(
        left_rows, right_rows, (((0, 2), (0, 2)), ((), ())), preferred_element_type=jnp.float32
    ) * scaling
    covariance_t = lax.dot_general(
        right_rows, left_rows, (((0, 2), (0, 2)), ((), ())), preferred_element_type=jnp.float32
    ) * scaling

    def cov_times(block, on_rows):
        if on_rows:
            partial_image = jnp.dot(
                covariance, block, precision=lax.Precision.HIGHEST,
                preferred_element_type=jnp.float32,
            )
            return _pair_split_sum(partial_image, "row")
        partial_image = jnp.dot(
            covariance_t, block, precision=lax.Precision.HIGHEST,
            preferred_element_type=jnp.float32,
        )
        return _halving_sum(partial_image, "col")

    basis_rows = lax.dynamic_slice_in_dim(start_basis, row_here * rows_here, rows_here, 0)
    image = cov_times(basis_rows, True)
    on_rows = False
    for sweep_index in range(ITERS):
        lower_factor = _lower_factor(image, "row" if on_rows else "col")
        if sweep_index == ITERS - 1:
            basis_rows = _right_solve(lower_factor, image)
            break
        image = _right_solve(lower_factor, cov_times(image, on_rows))
        on_rows = not on_rows
    if not on_rows:
        swapped = lax.ppermute(basis_rows, ("row", "col"), _transpose_pairs(row_count, col_count))
        basis_rows = jnp.where(row_here == col_here, basis_rows, swapped)
    out_rows = array_size // (row_count * col_count)
    basis_out = lax.dynamic_slice_in_dim(basis_rows, col_here * out_rows, out_rows, 0) * math.sqrt(array_size)
    return (covariance, basis_out)


def solution(mesh):
    in_specs = (P("row", "bin", "col"), P("bin", "row", None), P("bin", "row", None), P())
    out_specs = (P("col", "row"), P(("row", "col"), None))
    return jax.shard_map(shards, mesh=mesh, in_specs=in_specs, out_specs=out_specs, check_vma=False)
```

```python
import math

import jax
import jax.numpy as jnp
from jax import lax
from jax.sharding import PartitionSpec as P

ITERS = 2


def _transpose_pairs(row_count, col_count):
    return [
        (i * col_count + j, j * row_count + i)
        for i in range(row_count)
        for j in range(col_count)
        if i != j
    ]


def _butterfly_sum(x, axis):
    count = lax.axis_size(axis)
    if count & (count - 1):
        return lax.psum(x, axis)
    step = 1
    while step < count:
        x = x + lax.ppermute(x, axis, [(i, i ^ step) for i in range(count)])
        step *= 2
    return x


def _bits(count, far_first):
    steps = []
    step = 1
    while step < count:
        steps.append(step)
        step *= 2
    return steps[::-1] if far_first else steps


def _direct_sum(x, axis):
    count = lax.axis_size(axis)
    if count != 4:
        return _butterfly_sum(x, axis)
    got = [lax.ppermute(x, axis, [(i, i ^ k) for i in range(count)]) for k in (1, 2, 3)]
    return (x + got[0]) + (got[1] + got[2])


def _butterfly_gather(x, plan):
    x = x[None]
    for axis, step, slot in plan:
        count = lax.axis_size(axis)
        low = (lax.axis_index(axis) & step) == 0
        other = lax.ppermute(x, axis, [(i, i ^ step) for i in range(count)])
        below = 2 ** sum(1 for _, _, done in plan[: plan.index((axis, step, slot))] if done < slot)
        mine = x.reshape((-1, 1, below) + x.shape[1:])
        theirs = other.reshape(mine.shape)
        first = jnp.where(low, 0, 1)
        both = jnp.zeros((mine.shape[0], 2) + mine.shape[2:], x.dtype)
        both = lax.dynamic_update_slice_in_dim(both, mine, first, 1)
        both = lax.dynamic_update_slice_in_dim(both, theirs, 1 - first, 1)
        x = both.reshape((-1,) + x.shape[1:])
    return x


def _halving_sum(x, axis):
    count = lax.axis_size(axis)
    if count & (count - 1) or x.shape[0] % count:
        return _butterfly_sum(x, axis)
    here = lax.axis_index(axis)
    steps = _bits(count, False)
    for step in steps:
        half = x.shape[0] // 2
        low = (here & step) == 0
        keep = jnp.where(low, x[:half], x[half:])
        give = jnp.where(low, x[half:], x[:half])
        x = keep + lax.ppermute(give, axis, [(i, i ^ step) for i in range(count)])
    for step in steps[::-1]:
        low = (here & step) == 0
        other = lax.ppermute(x, axis, [(i, i ^ step) for i in range(count)])
        first = jnp.where(low, 0, x.shape[0])
        both = jnp.zeros((2 * x.shape[0],) + x.shape[1:], x.dtype)
        both = lax.dynamic_update_slice_in_dim(both, x, first, 0)
        x = lax.dynamic_update_slice_in_dim(both, other, x.shape[0] - first, 0)
    return x


def _pair_split_sum(x, axis):
    count = lax.axis_size(axis)
    if count != 4 or x.shape[0] % 2:
        return _butterfly_sum(x, axis)
    pairs = [(i, i ^ 1) for i in range(count)]
    near_low = (lax.axis_index(axis) & 1) == 0
    x = x + lax.ppermute(x, axis, pairs)
    half = x.shape[0] // 2
    mine = jnp.where(near_low, x[:half], x[half:])
    mine = mine + lax.ppermute(mine, axis, [(i, i ^ 2) for i in range(count)])
    other = lax.ppermute(mine, axis, pairs)
    first = jnp.where(near_low, 0, half)
    both = jnp.zeros(x.shape, x.dtype)
    both = lax.dynamic_update_slice_in_dim(both, mine, first, 0)
    return lax.dynamic_update_slice_in_dim(both, other, half - first, 0)


def _lower_factor(image, gram_axis):
    gram_part = jnp.dot(
        image.T, image, precision=lax.Precision.HIGHEST, preferred_element_type=jnp.float32
    )
    return lax.linalg.cholesky(_direct_sum(gram_part, gram_axis), symmetrize_input=False)


def _right_solve(lower_factor, image):
    return jax.scipy.linalg.solve_triangular(lower_factor, image.T, lower=True).T


def shards(snapshots, focus_in, focus_out, start_basis):
    rows_here, bins_here, snaps_here = snapshots.shape
    bin_count = lax.axis_size("bin")
    row_count = lax.axis_size("row")
    col_count = lax.axis_size("col")
    col_here = lax.axis_index("col")
    row_here = lax.axis_index("row")
    partial_proj = jnp.einsum(
        "mbs,bmr->brs", snapshots, focus_in, preferred_element_type=jnp.float32
    )
    projected = _direct_sum(partial_proj, "row").astype(jnp.bfloat16)
    lifted = jnp.einsum("bmr,brs->mbs", focus_out, projected, preferred_element_type=jnp.float32)
    focused = (snapshots.astype(jnp.float32) + lifted).astype(jnp.bfloat16)
    columns = bins_here * snaps_here
    local_rows = focused.reshape(rows_here, columns)
    array_size = rows_here * row_count
    col_block = array_size // col_count
    scaling = 1.0 / (columns * col_count * bin_count)

    power_of_two = all(n & (n - 1) == 0 for n in (bin_count, row_count, col_count))
    if row_count == col_count and power_of_two:
        swapped = lax.ppermute(local_rows, ("row", "col"), _transpose_pairs(row_count, col_count))
        swapped = jnp.where(row_here == col_here, local_rows, swapped)
        group = _bits(col_count, True)
        bins = _bits(bin_count, True)
        right_plan = [("col", step, k) for k, step in enumerate(group)]
        right_plan += [("bin", step, len(group) + k) for k, step in enumerate(bins)]
        left_plan = [("bin", step, len(group) + k) for k, step in enumerate(bins)]
        left_plan += [("row", step, k) for k, step in enumerate(group)]
        half = rows_here // 2
        early_bin = [step for step in right_plan if step[0] == "bin"]
        early_bin += [step for step in right_plan if step[0] != "bin"]
        right_rows = jnp.concatenate(
            [
                _butterfly_gather(local_rows[:half], right_plan),
                _butterfly_gather(local_rows[half:], early_bin),
            ],
            1,
        )
        left_rows = jnp.concatenate(
            [
                _butterfly_gather(swapped[:half], left_plan),
                _butterfly_gather(swapped[half:], left_plan),
            ],
            1,
        )
    else:
        right_rows = lax.all_gather(local_rows, ("bin", "col"), axis=0, tiled=False)
        every_row = lax.all_gather(right_rows, "row", axis=1, tiled=True)
        left_rows = lax.dynamic_slice_in_dim(every_row, col_here * col_block, col_block, 1)
    covariance = lax.dot_general(
        left_rows, right_rows, (((0, 2), (0, 2)), ((), ())), preferred_element_type=jnp.float32
    ) * scaling
    covariance_t = lax.dot_general(
        right_rows, left_rows, (((0, 2), (0, 2)), ((), ())), preferred_element_type=jnp.float32
    ) * scaling

    def cov_times(block, on_rows):
        if on_rows:
            partial_image = jnp.dot(
                covariance, block, precision=lax.Precision.HIGHEST,
                preferred_element_type=jnp.float32,
            )
            return _pair_split_sum(partial_image, "row")
        partial_image = jnp.dot(
            covariance_t, block, precision=lax.Precision.HIGHEST,
            preferred_element_type=jnp.float32,
        )
        return _halving_sum(partial_image, "col")

    basis_rows = lax.dynamic_slice_in_dim(start_basis, row_here * rows_here, rows_here, 0)
    image = cov_times(basis_rows, True)
    on_rows = False
    for sweep_index in range(ITERS):
        lower_factor = _lower_factor(image, "row" if on_rows else "col")
        if sweep_index == ITERS - 1:
            basis_rows = _right_solve(lower_factor, image)
            break
        image = _right_solve(lower_factor, cov_times(image, on_rows))
        on_rows = not on_rows
    if not on_rows:
        swapped = lax.ppermute(basis_rows, ("row", "col"), _transpose_pairs(row_count, col_count))
        basis_rows = jnp.where(row_here == col_here, basis_rows, swapped)
    out_rows = array_size // (row_count * col_count)
    basis_out = lax.dynamic_slice_in_dim(basis_rows, col_here * out_rows, out_rows, 0) * math.sqrt(array_size)
    return (covariance, basis_out)


def solution(mesh):
    in_specs = (P("row", "bin", "col"), P("bin", "row", None), P("bin", "row", None), P())
    out_specs = (P("col", "row"), P(("row", "col"), None))
    return jax.shard_map(shards, mesh=mesh, in_specs=in_specs, out_specs=out_specs, check_vma=False)
```

```python
import math

import jax
import jax.numpy as jnp
from jax import lax
from jax.sharding import PartitionSpec as P

ITERS = 2


def _transpose_pairs(row_count, col_count):
    return [
        (i * col_count + j, j * row_count + i)
        for i in range(row_count)
        for j in range(col_count)
        if i != j
    ]


def _butterfly_sum(x, axis):
    count = lax.axis_size(axis)
    if count & (count - 1):
        return lax.psum(x, axis)
    step = 1
    while step < count:
        x = x + lax.ppermute(x, axis, [(i, i ^ step) for i in range(count)])
        step *= 2
    return x


def _bits(count, far_first):
    steps = []
    step = 1
    while step < count:
        steps.append(step)
        step *= 2
    return steps[::-1] if far_first else steps


def _direct_sum(x, axis):
    count = lax.axis_size(axis)
    if count != 4:
        return _butterfly_sum(x, axis)
    got = [lax.ppermute(x, axis, [(i, i ^ k) for i in range(count)]) for k in (1, 2, 3)]
    return (x + got[0]) + (got[1] + got[2])


def _butterfly_gather(x, plan):
    x = x[None]
    for axis, step, slot in plan:
        count = lax.axis_size(axis)
        low = (lax.axis_index(axis) & step) == 0
        other = lax.ppermute(x, axis, [(i, i ^ step) for i in range(count)])
        below = 2 ** sum(1 for _, _, done in plan[: plan.index((axis, step, slot))] if done < slot)
        mine = x.reshape((-1, 1, below) + x.shape[1:])
        theirs = other.reshape(mine.shape)
        first = jnp.where(low, 0, 1)
        both = jnp.zeros((mine.shape[0], 2) + mine.shape[2:], x.dtype)
        both = lax.dynamic_update_slice_in_dim(both, mine, first, 1)
        both = lax.dynamic_update_slice_in_dim(both, theirs, 1 - first, 1)
        x = both.reshape((-1,) + x.shape[1:])
    return x


def _halving_sum(x, axis):
    count = lax.axis_size(axis)
    if count & (count - 1) or x.shape[0] % count:
        return _butterfly_sum(x, axis)
    here = lax.axis_index(axis)
    steps = _bits(count, False)
    for step in steps:
        half = x.shape[0] // 2
        low = (here & step) == 0
        keep = jnp.where(low, x[:half], x[half:])
        give = jnp.where(low, x[half:], x[:half])
        x = keep + lax.ppermute(give, axis, [(i, i ^ step) for i in range(count)])
    for step in steps[::-1]:
        low = (here & step) == 0
        other = lax.ppermute(x, axis, [(i, i ^ step) for i in range(count)])
        first = jnp.where(low, 0, x.shape[0])
        both = jnp.zeros((2 * x.shape[0],) + x.shape[1:], x.dtype)
        both = lax.dynamic_update_slice_in_dim(both, x, first, 0)
        x = lax.dynamic_update_slice_in_dim(both, other, x.shape[0] - first, 0)
    return x


def _pair_split_sum(x, axis):
    count = lax.axis_size(axis)
    if count != 4 or x.shape[0] % 2:
        return _butterfly_sum(x, axis)
    pairs = [(i, i ^ 1) for i in range(count)]
    near_low = (lax.axis_index(axis) & 1) == 0
    x = x + lax.ppermute(x, axis, pairs)
    half = x.shape[0] // 2
    mine = jnp.where(near_low, x[:half], x[half:])
    mine = mine + lax.ppermute(mine, axis, [(i, i ^ 2) for i in range(count)])
    other = lax.ppermute(mine, axis, pairs)
    first = jnp.where(near_low, 0, half)
    both = jnp.zeros(x.shape, x.dtype)
    both = lax.dynamic_update_slice_in_dim(both, mine, first, 0)
    return lax.dynamic_update_slice_in_dim(both, other, half - first, 0)


def _lower_factor(image, gram_axis):
    gram_part = jnp.dot(
        image.T, image, precision=lax.Precision.HIGHEST, preferred_element_type=jnp.float32
    )
    return jnp.linalg.cholesky(_direct_sum(gram_part, gram_axis))


def _right_solve(lower_factor, image):
    return jax.scipy.linalg.solve_triangular(lower_factor, image.T, lower=True).T


def shards(snapshots, focus_in, focus_out, start_basis):
    rows_here, bins_here, snaps_here = snapshots.shape
    bin_count = lax.axis_size("bin")
    row_count = lax.axis_size("row")
    col_count = lax.axis_size("col")
    col_here = lax.axis_index("col")
    row_here = lax.axis_index("row")
    partial_proj = jnp.einsum(
        "mbs,bmr->brs", snapshots, focus_in, preferred_element_type=jnp.float32
    )
    projected = _direct_sum(partial_proj, "row").astype(jnp.bfloat16)
    lifted = jnp.einsum("bmr,brs->mbs", focus_out, projected, preferred_element_type=jnp.float32)
    focused = (snapshots.astype(jnp.float32) + lifted).astype(jnp.bfloat16)
    columns = bins_here * snaps_here
    local_rows = focused.reshape(rows_here, columns)
    array_size = rows_here * row_count
    col_block = array_size // col_count
    scaling = 1.0 / (columns * col_count * bin_count)

    power_of_two = all(n & (n - 1) == 0 for n in (bin_count, row_count, col_count))
    if row_count == col_count and power_of_two:
        swapped = lax.ppermute(local_rows, ("row", "col"), _transpose_pairs(row_count, col_count))
        swapped = jnp.where(row_here == col_here, local_rows, swapped)
        group = _bits(col_count, True)
        bins = _bits(bin_count, True)
        right_plan = [("col", step, k) for k, step in enumerate(group)]
        right_plan += [("bin", step, len(group) + k) for k, step in enumerate(bins)]
        left_plan = [("bin", step, len(group) + k) for k, step in enumerate(bins)]
        left_plan += [("row", step, k) for k, step in enumerate(group)]
        half = rows_here // 2
        early_bin = [step for step in right_plan if step[0] == "bin"]
        early_bin += [step for step in right_plan if step[0] != "bin"]
        right_rows = jnp.concatenate(
            [
                _butterfly_gather(local_rows[:half], right_plan),
                _butterfly_gather(local_rows[half:], early_bin),
            ],
            1,
        )
        left_rows = jnp.concatenate(
            [
                _butterfly_gather(swapped[:half], left_plan),
                _butterfly_gather(swapped[half:], left_plan),
            ],
            1,
        )
    else:
        right_rows = lax.all_gather(local_rows, ("bin", "col"), axis=0, tiled=False)
        every_row = lax.all_gather(right_rows, "row", axis=1, tiled=True)
        left_rows = lax.dynamic_slice_in_dim(every_row, col_here * col_block, col_block, 1)
    covariance = lax.dot_general(
        left_rows, right_rows, (((0, 2), (0, 2)), ((), ())), preferred_element_type=jnp.float32
    ) * scaling
    covariance_t = covariance.T

    def cov_times(block, on_rows):
        if on_rows:
            partial_image = jnp.dot(
                covariance, block, precision=lax.Precision.HIGHEST,
                preferred_element_type=jnp.float32,
            )
            return _pair_split_sum(partial_image, "row")
        partial_image = jnp.dot(
            covariance_t, block, precision=lax.Precision.HIGHEST,
            preferred_element_type=jnp.float32,
        )
        return _halving_sum(partial_image, "col")

    basis_rows = lax.dynamic_slice_in_dim(start_basis, row_here * rows_here, rows_here, 0)
    image = cov_times(basis_rows, True)
    on_rows = False
    for sweep_index in range(ITERS):
        lower_factor = _lower_factor(image, "row" if on_rows else "col")
        if sweep_index == ITERS - 1:
            basis_rows = _right_solve(lower_factor, image)
            break
        image = _right_solve(lower_factor, cov_times(image, on_rows))
        on_rows = not on_rows
    if not on_rows:
        swapped = lax.ppermute(basis_rows, ("row", "col"), _transpose_pairs(row_count, col_count))
        basis_rows = jnp.where(row_here == col_here, basis_rows, swapped)
    out_rows = array_size // (row_count * col_count)
    basis_out = lax.dynamic_slice_in_dim(basis_rows, col_here * out_rows, out_rows, 0) * math.sqrt(array_size)
    return (covariance, basis_out)


def solution(mesh):
    in_specs = (P("row", "bin", "col"), P("bin", "row", None), P("bin", "row", None), P())
    out_specs = (P("col", "row"), P(("row", "col"), None))
    return jax.shard_map(shards, mesh=mesh, in_specs=in_specs, out_specs=out_specs, check_vma=False)
```
